512 devices in a mesh: ctx: 256 (over z, y, x_lo, core), kvh: 2 (over x_hi).
Axes of the slice: x: 4 (x_hi: 2, x_lo: 2; x = x_hi * 2 + x_lo), y: 8, z: 8, core: 2. Of those that a mesh axis runs over, the one named last changes fastest.
Arguments:
- queries: bfloat16 [65536, 64, 128], P('ctx', 'kvh'), may hold values from -110 to 110
- key_value: bfloat16 [2, 65536, 8, 128], P(None, 'ctx', 'kvh'), may hold values from -5 to 5
- span_table: int32 [512], replicated, may hold values from 0 to 511, as said below
Outputs:
- attended: bfloat16 [65536, 8192], P(('ctx', 'kvh'))
The draws below stay inside these ranges and needn't reach their ends.
Inputs may be any that keep to these rules, and one draw needn't show every extreme that they name: `span_table`: entries 2 d and 2 d + 1 are the spans of ctx index d: the first below 256, the second 256 or above; every span of 0 to 511 appears exactly once.
All inputs are finite; a program needn't handle non-finite values.
Results may differ from the reference program's by a relative error of at most 0.0065.
Values may be sent and summed in bfloat16 or wider, within the bound.
No kernel may reach another device: no remote copies, remote signals or barrier semaphores. Data moves between devices by JAX's collectives and lax.ppermute only.
A program may use at most 64 MiB of HBM per device.

```python
import jax
import jax.numpy as jnp
from jax import lax

QH = 64
KVH = 8
HD = 128
CH = 128
STEPS = 4
TOKENS = 65536
N_CTX = 256


def base_keys(key):
    base = jax.random.normal(jax.random.fold_in(key, 11), (TOKENS, KVH, HD), jnp.float32)
    return jnp.clip(base, -4.5, 4.5)


def draw_key_value(key, part):
    base = base_keys(key)
    keys = base
    vals = jnp.clip(jax.random.normal(jax.random.fold_in(key, 14), (TOKENS, KVH, HD), jnp.float32), -4.5, 4.5)
    return jnp.stack([keys, vals]).astype(jnp.bfloat16)


def draw_queries(key, part):
    drawn = jnp.clip(jax.random.normal(jax.random.fold_in(key, 13), (TOKENS, QH, HD), jnp.float32), -4.5, 4.5)
    result = drawn
    return result.astype(jnp.bfloat16)


def draw_span_table(key, part):
    early = jax.random.permutation(jax.random.fold_in(key, 21), N_CTX).astype(jnp.int32)
    late = N_CTX + jax.random.permutation(jax.random.fold_in(key, 22), N_CTX).astype(jnp.int32)
    return jnp.stack([early, late], axis=1).reshape(2 * N_CTX).astype(jnp.int32)


def setup_inputs(seed: int = 0) -> dict:
    arg_keys = jax.random.split(jax.random.key(seed), 4)
    queries = draw_queries(jax.random.fold_in(arg_keys[3], 71), 0)
    key_value = draw_key_value(jax.random.fold_in(arg_keys[3], 71), 0)
    span_table = draw_span_table(jax.random.fold_in(arg_keys[3], 71), 0)
    return {"queries": queries, "key_value": key_value, "span_table": span_table}


def reference(queries, key_value, span_table):
    rows = 2 * CH
    group = QH // KVH
    scale = 1.0 / (HD ** 0.5)
    offsets = jnp.arange(CH, dtype=jnp.int32)
    positions = (span_table[:, None] * CH + offsets[None, :]).reshape(N_CTX, rows).astype(jnp.int32)
    qall = queries.reshape(N_CTX, rows, KVH, group, HD)
    kall = key_value[0].reshape(N_CTX, rows, KVH, HD)
    vall = key_value[1].reshape(N_CTX, rows, KVH, HD)

    def one_device(dev):
        qdev = lax.dynamic_index_in_dim(qall, dev, 0, keepdims=False).astype(jnp.float32)
        qpos = lax.dynamic_index_in_dim(positions, dev, 0, keepdims=False)
        maxima = []
        outs = []
        sums = []
        for dist in range(STEPS):
            src = ((dev - dist) % N_CTX).astype(jnp.int32)
            kdev = lax.dynamic_index_in_dim(kall, src, 0, keepdims=False).astype(jnp.float32)
            vdev = lax.dynamic_index_in_dim(vall, src, 0, keepdims=False).astype(jnp.float32)
            kpos = lax.dynamic_index_in_dim(positions, src, 0, keepdims=False)
            scores = jnp.einsum("qghd,kgd->ghqk", qdev, kdev) * scale
            visible = (kpos[None, :] <= qpos[:, None])[None, None]
            masked = jnp.where(visible, scores, -jnp.inf)
            block_max = jnp.maximum(jnp.max(masked, axis=-1), jnp.float32(-1e30))
            weight = jnp.exp(masked - block_max[..., None])
            weight_low = weight.astype(jnp.bfloat16).astype(jnp.float32)
            sums.append(jnp.sum(weight, axis=-1))
            outs.append(jnp.einsum("ghqk,kgd->ghqd", weight_low, vdev))
            maxima.append(block_max)
        top = maxima[0]
        for m in maxima[1:]:
            top = jnp.maximum(top, m)
        numer = jnp.zeros_like(outs[0])
        denom = jnp.zeros_like(sums[0])
        for m, o, s in zip(maxima, outs, sums):
            factor = jnp.exp(m - top)
            numer = numer + factor[..., None] * o
            denom = denom + factor * s
        result = numer / denom[..., None]
        return jnp.transpose(result, (2, 0, 1, 3)).reshape(rows, QH * HD).astype(jnp.bfloat16)

    stacked = lax.map(one_device, jnp.arange(N_CTX, dtype=jnp.int32))
    return stacked.reshape(TOKENS, QH * HD)
```

```python
import functools

import jax
import jax.numpy as jnp
from jax import lax
from jax.experimental import pallas as pl
from jax.experimental.pallas import tpu as pltpu
from jax.sharding import PartitionSpec as P

STEPS = 4


def shifted(value, axis, steps):
    count = lax.axis_size(axis)
    pairs = [(source, (source + steps) % count) for source in range(count)]
    return lax.ppermute(value, axis, pairs)


def attend_kernel(info_ref, q_ref, *refs, span, group, head_size, steps, scale):
    kv_refs = refs[:steps]
    o_ref = refs[steps]
    m_ref, l_ref, acc_ref = refs[steps + 1 :]
    query_span = info_ref[1]

    m_ref[...] = jnp.full(m_ref.shape, -jnp.inf, jnp.float32)
    l_ref[...] = jnp.zeros(l_ref.shape, jnp.float32)
    acc_ref[...] = jnp.zeros(acc_ref.shape, jnp.float32)

    row = lax.broadcasted_iota(jnp.int32, (span, span), 0)
    col = lax.broadcasted_iota(jnp.int32, (span, span), 1)

    def run(kv_ref, t, masked):
        k = kv_ref[0, t * span : (t + 1) * span, :]
        v = kv_ref[1, t * span : (t + 1) * span, :]

        def head(h, carry):
            off = pl.multiple_of(h * head_size, head_size)
            qv = q_ref[:, pl.ds(off, head_size)]
            s = lax.dot_general(
                qv, k, (((1,), (1,)), ((), ())), preferred_element_type=jnp.float32
            ) * scale
            if masked:
                s = jnp.where(col <= row, s, -jnp.inf)
            m_old = m_ref[h]
            m_new = jnp.maximum(m_old, jnp.max(s, axis=1, keepdims=True))
            p = jnp.exp(s - m_new)
            alpha = jnp.exp(m_old - m_new)
            l_ref[h] = alpha * l_ref[h] + jnp.sum(p, axis=1, keepdims=True)
            acc_ref[h] = alpha * acc_ref[h] + jnp.dot(
                p.astype(jnp.bfloat16), v, preferred_element_type=jnp.float32
            )
            m_ref[h] = m_new
            return carry

        lax.fori_loop(0, group, head, 0)

    for b in range(steps):
        for t in range(2):
            key_span = info_ref[2 + 2 * b + t]

            @pl.when(key_span < query_span)
            def _(b=b, t=t):
                run(kv_refs[b], t, False)

            @pl.when(key_span == query_span)
            def _(b=b, t=t):
                run(kv_refs[b], t, True)

    def finish(h, carry):
        off = pl.multiple_of(h * head_size, head_size)
        o_ref[:, pl.ds(off, head_size)] = (acc_ref[h] / l_ref[h]).astype(o_ref.dtype)
        return carry

    lax.fori_loop(0, group, finish, 0)


def attend_half(info, q2, blocks, *, span, group, kv_here, head_size, out_cols, out_block0):
    steps = len(blocks)
    width = group * head_size
    kernel = functools.partial(
        attend_kernel,
        span=span,
        group=group,
        head_size=head_size,
        steps=steps,
        scale=1.0 / head_size**0.5,
    )
    q_spec = pl.BlockSpec((span, width), lambda g, info: (info[0], g))
    kv_spec = pl.BlockSpec((2, 2 * span, head_size), lambda g, info: (0, 0, g))
    o_spec = pl.BlockSpec((span, width), lambda g, info: (0, out_block0(info) + g))
    flops = 4 * span * 2 * span * steps * head_size * group * kv_here
    return pl.pallas_call(
        kernel,
        out_shape=jax.ShapeDtypeStruct((span, out_cols), jnp.bfloat16),
        grid_spec=pltpu.PrefetchScalarGridSpec(
            num_scalar_prefetch=1,
            grid=(kv_here,),
            in_specs=[q_spec] + [kv_spec] * steps,
            out_specs=o_spec,
            scratch_shapes=[
                pltpu.VMEM((group, span, 1), jnp.float32),
                pltpu.VMEM((group, span, 1), jnp.float32),
                pltpu.VMEM((group, span, head_size), jnp.float32),
            ],
        ),
        compiler_params=pltpu.CompilerParams(dimension_semantics=("arbitrary",)),
        cost_estimate=pl.CostEstimate(
            flops=flops,
            transcendentals=flops // (4 * head_size),
            bytes_accessed=2 * span * width * kv_here * 2 + steps * 2 * 2 * span * kv_here * head_size * 2,
        ),
    )(info, q2, *blocks)


def body(queries, key_value, span_table):
    rows = queries.shape[0]
    heads_here = queries.shape[1]
    head_size = queries.shape[2]
    kv_here = key_value.shape[2]
    group = heads_here // kv_here
    span = rows // 2
    cycle = lax.axis_size("ctx")
    myself = lax.axis_index("ctx")
    half = lax.axis_index("kvh")
    table = span_table.reshape(cycle, 2)

    q2 = queries.reshape(rows, heads_here * head_size)
    own = key_value.reshape(2, rows, kv_here * head_size)
    blocks = [own] + [shifted(own, "ctx", d) for d in range(1, STEPS)]

    sources = (myself - jnp.arange(STEPS, dtype=jnp.int32)) % cycle
    key_spans = table[sources].reshape(2 * STEPS)

    def info_for(qh):
        return jnp.concatenate(
            [jnp.stack([qh, table[myself, qh]]).astype(jnp.int32), key_spans]
        )

    width = heads_here * head_size
    sent_info = info_for(1 - half)
    kept_info = info_for(half)
    common = dict(span=span, group=group, kv_here=kv_here, head_size=head_size)
    sent = attend_half(sent_info, q2, blocks, out_cols=width, out_block0=lambda i: 0, **common)
    arrived = shifted(sent, "kvh", 1)
    out = attend_half(
        kept_info,
        q2,
        blocks,
        out_cols=2 * width,
        out_block0=lambda i: i[0] * kv_here,
        **common,
    )
    return lax.dynamic_update_slice(out, arrived, (0, (1 - half) * width))


def solution(mesh):
    in_specs = (P("ctx", "kvh", None), P(None, "ctx", "kvh", None), P())
    out_specs = P(("ctx", "kvh"), None)
    return jax.shard_map(body, mesh=mesh, in_specs=in_specs, out_specs=out_specs, check_vma=False)
```

```python
import functools

import jax
import jax.numpy as jnp
from jax import lax
from jax.experimental import pallas as pl
from jax.experimental.pallas import tpu as pltpu
from jax.sharding import PartitionSpec as P

STEPS = 4


def shifted(value, axis, steps):
    count = lax.axis_size(axis)
    pairs = [(source, (source + steps) % count) for source in range(count)]
    return lax.ppermute(value, axis, pairs)


def attend_kernel(info_ref, q_ref, *refs, span, group, head_size, steps, scale):
    kv_refs = refs[:steps]
    o_ref = refs[steps]
    s_ref, mx_ref, sm_ref, acc_ref = refs[steps + 1 :]
    query_span = info_ref[1]
    n = group * span

    mx_ref[...] = jnp.full(mx_ref.shape, -jnp.inf, jnp.float32)
    tiles = [(b, t) for b in range(steps) for t in range(2)]

    def score(idx, b, t, masked):
        k = kv_refs[b][0, t * span : (t + 1) * span, :]
        q = q_ref[...].reshape(n, head_size)
        s = lax.dot_general(
            q, k, (((1,), (1,)), ((), ())), preferred_element_type=jnp.float32
        ) * scale
        if masked:
            row = lax.broadcasted_iota(jnp.int32, (n, span), 0) % span
            col = lax.broadcasted_iota(jnp.int32, (n, span), 1)
            s = jnp.where(col <= row, s, -jnp.inf)
        s_ref[idx] = s
        mx_ref[...] = jnp.maximum(mx_ref[...], s)

    for idx, (b, t) in enumerate(tiles):
        key_span = info_ref[2 + idx]
        pl.when(key_span < query_span)(functools.partial(score, idx, b, t, False))
        if b == 0:
            pl.when(key_span == query_span)(functools.partial(score, idx, b, t, True))

    m = jnp.max(mx_ref[...], axis=1, keepdims=True)
    mx_ref[...] = jnp.broadcast_to(m, (n, span))
    sm_ref[...] = jnp.zeros(sm_ref.shape, jnp.float32)
    acc_ref[...] = jnp.zeros(acc_ref.shape, jnp.float32)

    def weigh(idx, b, t):
        p = jnp.exp(s_ref[idx] - mx_ref[...])
        sm_ref[...] += p
        v = kv_refs[b][1, t * span : (t + 1) * span, :]
        acc_ref[...] += jnp.dot(p.astype(jnp.bfloat16), v, preferred_element_type=jnp.float32)

    for idx, (b, t) in enumerate(tiles):
        key_span = info_ref[2 + idx]
        pl.when(key_span <= query_span)(functools.partial(weigh, idx, b, t))

    total = jnp.sum(sm_ref[...], axis=1, keepdims=True)
    result = acc_ref[...] / total
    for h in range(group):
        o_ref[:, h * head_size : (h + 1) * head_size] = result[
            h * span : (h + 1) * span, :
        ].astype(o_ref.dtype)


def attend_half(info, q2, blocks, *, span, group, kv_here, head_size, out_cols, out_block0):
    steps = len(blocks)
    width = group * head_size
    kernel = functools.partial(
        attend_kernel,
        span=span,
        group=group,
        head_size=head_size,
        steps=steps,
        scale=1.0 / head_size**0.5,
    )
    q_spec = pl.BlockSpec((group, span, head_size), lambda g, info: (g, info[0], 0))
    kv_spec = pl.BlockSpec((2, 2 * span, head_size), lambda g, info: (0, 0, g))
    o_spec = pl.BlockSpec((span, width), lambda g, info: (0, out_block0(info) + g))
    flops = 4 * span * 2 * span * steps * head_size * group * kv_here
    return pl.pallas_call(
        kernel,
        out_shape=jax.ShapeDtypeStruct((span, out_cols), jnp.bfloat16),
        grid_spec=pltpu.PrefetchScalarGridSpec(
            num_scalar_prefetch=1,
            grid=(kv_here,),
            in_specs=[q_spec] + [kv_spec] * steps,
            out_specs=o_spec,
            scratch_shapes=[
                pltpu.VMEM((2 * steps, group * span, span), jnp.float32),
                pltpu.VMEM((group * span, span), jnp.float32),
                pltpu.VMEM((group * span, span), jnp.float32),
                pltpu.VMEM((group * span, head_size), jnp.float32),
            ],
        ),
        compiler_params=pltpu.CompilerParams(dimension_semantics=("arbitrary",)),
        cost_estimate=pl.CostEstimate(
            flops=flops,
            transcendentals=flops // (4 * head_size),
            bytes_accessed=2 * span * width * kv_here * 2 + steps * 2 * 2 * span * kv_here * head_size * 2,
        ),
    )(info, q2, *blocks)


def body(queries, key_value, span_table):
    rows = queries.shape[0]
    heads_here = queries.shape[1]
    head_size = queries.shape[2]
    kv_here = key_value.shape[2]
    group = heads_here // kv_here
    span = rows // 2
    cycle = lax.axis_size("ctx")
    myself = lax.axis_index("ctx")
    half = lax.axis_index("kvh")
    table = span_table.reshape(cycle, 2)

    q2 = jnp.transpose(queries, (1, 0, 2))
    own = key_value.reshape(2, rows, kv_here * head_size)
    first = shifted(own, "ctx", 1)
    third = shifted(own, "ctx", 3)
    pairs = [(d, d ^ 1) for d in range(cycle)]
    second = lax.ppermute(jnp.where(myself % 2 == 0, first, third), "ctx", pairs)
    blocks = [own, first, second, third]

    sources = (myself - jnp.arange(STEPS, dtype=jnp.int32)) % cycle
    key_spans = table[sources].reshape(2 * STEPS)

    def info_for(qh):
        return jnp.concatenate(
            [jnp.stack([qh, table[myself, qh]]).astype(jnp.int32), key_spans]
        )

    width = heads_here * head_size
    sent_info = info_for(1 - half)
    kept_info = info_for(half)
    common = dict(span=span, group=group, kv_here=kv_here, head_size=head_size)
    sent = attend_half(sent_info, q2, blocks, out_cols=width, out_block0=lambda i: 0, **common)
    arrived = shifted(sent, "kvh", 1)
    out = attend_half(
        kept_info,
        q2,
        blocks,
        out_cols=2 * width,
        out_block0=lambda i: i[0] * kv_here,
        **common,
    )
    return lax.dynamic_update_slice(out, arrived, (0, (1 - half) * width))


def solution(mesh):
    in_specs = (P("ctx", "kvh", None), P(None, "ctx", "kvh", None), P())
    out_specs = P(("ctx", "kvh"), None)
    return jax.shard_map(body, mesh=mesh, in_specs=in_specs, out_specs=out_specs, check_vma=False)
```

```python
import functools

import jax
import jax.numpy as jnp
from jax import lax
from jax.experimental import pallas as pl
from jax.experimental.pallas import tpu as pltpu
from jax.sharding import PartitionSpec as P

STEPS = 4


def shifted(value, axis, steps):
    count = lax.axis_size(axis)
    pairs = [(source, (source + steps) % count) for source in range(count)]
    return lax.ppermute(value, axis, pairs)


def attend_kernel(table_ref, where_ref, q_ref, *refs, span, group, head_size, steps, scale):
    kv_refs = refs[:steps]
    o_ref = refs[steps]
    s_ref, mx_ref, sm_ref, acc_ref = refs[steps + 1 :]
    cycle = table_ref.shape[0] // 2
    myself = where_ref[1]
    query_span = table_ref[2 * myself + where_ref[0]]
    key_spans = [
        table_ref[2 * ((myself + cycle - b) % cycle) + t] for b in range(steps) for t in range(2)
    ]
    n = group * span

    mx_ref[...] = jnp.full(mx_ref.shape, -jnp.inf, jnp.float32)
    tiles = [(b, t) for b in range(steps) for t in range(2)]

    def score(idx, b, t, masked):
        k = kv_refs[b][0, t * span : (t + 1) * span, :]
        q = q_ref[...].reshape(n, head_size)
        s = lax.dot_general(
            q, k, (((1,), (1,)), ((), ())), preferred_element_type=jnp.float32
        ) * scale
        if masked:
            row = lax.broadcasted_iota(jnp.int32, (n, span), 0) % span
            col = lax.broadcasted_iota(jnp.int32, (n, span), 1)
            s = jnp.where(col <= row, s, -jnp.inf)
        s_ref[idx] = s
        mx_ref[...] = jnp.maximum(mx_ref[...], s)

    for idx, (b, t) in enumerate(tiles):
        key_span = key_spans[idx]
        pl.when(key_span < query_span)(functools.partial(score, idx, b, t, False))
        if b == 0:
            pl.when(key_span == query_span)(functools.partial(score, idx, b, t, True))

    m = jnp.max(mx_ref[...], axis=1, keepdims=True)
    mx_ref[...] = jnp.broadcast_to(m, (n, span))
    sm_ref[...] = jnp.zeros(sm_ref.shape, jnp.float32)
    acc_ref[...] = jnp.zeros(acc_ref.shape, jnp.float32)

    def weigh(idx, b, t):
        p = jnp.exp(s_ref[idx] - mx_ref[...])
        sm_ref[...] += p
        v = kv_refs[b][1, t * span : (t + 1) * span, :]
        acc_ref[...] += jnp.dot(p.astype(jnp.bfloat16), v, preferred_element_type=jnp.float32)

    for idx, (b, t) in enumerate(tiles):
        key_span = key_spans[idx]
        pl.when(key_span <= query_span)(functools.partial(weigh, idx, b, t))

    total = jnp.sum(sm_ref[...], axis=1, keepdims=True)
    result = acc_ref[...] / total
    for h in range(group):
        o_ref[:, h * head_size : (h + 1) * head_size] = result[
            h * span : (h + 1) * span, :
        ].astype(o_ref.dtype)


def attend_half(table, where, q2, blocks, *, span, group, head_size, first, count, out_cols, out_block0):
    steps = len(blocks)
    width = group * head_size
    kernel = functools.partial(
        attend_kernel,
        span=span,
        group=group,
        head_size=head_size,
        steps=steps,
        scale=1.0 / head_size**0.5,
    )
    q_spec = pl.BlockSpec((group, span, head_size), lambda g, tb, w: (g + first, w[0], 0))
    kv_spec = pl.BlockSpec((2, 2 * span, head_size), lambda g, tb, w: (0, 0, g + first))
    o_spec = pl.BlockSpec((span, width), lambda g, tb, w: (0, out_block0(w) + g))
    flops = 4 * span * 2 * span * steps * head_size * group * count
    return pl.pallas_call(
        kernel,
        out_shape=jax.ShapeDtypeStruct((span, out_cols), jnp.bfloat16),
        grid_spec=pltpu.PrefetchScalarGridSpec(
            num_scalar_prefetch=2,
            grid=(count,),
            in_specs=[q_spec] + [kv_spec] * steps,
            out_specs=o_spec,
            scratch_shapes=[
                pltpu.VMEM((2 * steps, group * span, span), jnp.float32),
                pltpu.VMEM((group * span, span), jnp.float32),
                pltpu.VMEM((group * span, span), jnp.float32),
                pltpu.VMEM((group * span, head_size), jnp.float32),
            ],
        ),
        compiler_params=pltpu.CompilerParams(dimension_semantics=("arbitrary",)),
        cost_estimate=pl.CostEstimate(
            flops=flops,
            transcendentals=flops // (4 * head_size),
            bytes_accessed=2 * span * width * count * 2 + steps * 2 * 2 * span * count * head_size * 2,
        ),
    )(table, where, q2, *blocks)


def body(queries, key_value, span_table):
    rows = queries.shape[0]
    heads_here = queries.shape[1]
    head_size = queries.shape[2]
    kv_here = key_value.shape[2]
    group = heads_here // kv_here
    span = rows // 2
    cycle = lax.axis_size("ctx")
    myself = lax.axis_index("ctx")
    half = lax.axis_index("kvh")
    table = span_table.reshape(cycle, 2)

    q2 = jnp.transpose(queries, (1, 0, 2))
    own = key_value.reshape(2, rows, kv_here * head_size)
    first = shifted(own, "ctx", 1)
    third = shifted(own, "ctx", 3)
    pairs = [(d, d ^ 1) for d in range(cycle)]
    second = lax.ppermute(jnp.where(myself % 2 == 0, first, third), "ctx", pairs)
    blocks = [own, first, second, third]

    width = heads_here * head_size
    lanes = jnp.arange(2, dtype=jnp.int32)
    sent_where = jnp.where(lanes == 0, 1 - half, myself).astype(jnp.int32)
    kept_where = jnp.where(lanes == 0, half, myself).astype(jnp.int32)
    common = dict(span=span, group=group, head_size=head_size)
    chunks = 2
    per = kv_here // chunks
    arrived = []
    for j in range(chunks):
        sent = attend_half(
            span_table, sent_where, q2, blocks, first=j * per, count=per,
            out_cols=per * group * head_size, out_block0=lambda w: 0, **common,
        )
        arrived.append(shifted(sent, "kvh", 1))
    out = attend_half(
        span_table, kept_where, q2, blocks, first=0, count=kv_here,
        out_cols=2 * width, out_block0=lambda w: w[0] * kv_here, **common,
    )
    for j in range(chunks):
        out = lax.dynamic_update_slice(
            out, arrived[j], (0, (1 - half) * width + j * per * group * head_size)
        )
    return out


def solution(mesh):
    in_specs = (P("ctx", "kvh", None), P(None, "ctx", "kvh", None), P())
    out_specs = P(("ctx", "kvh"), None)
    return jax.shard_map(body, mesh=mesh, in_specs=in_specs, out_specs=out_specs, check_vma=False)
```

```python
import functools

import jax
import jax.numpy as jnp
from jax import lax
from jax.experimental import pallas as pl
from jax.experimental.pallas import tpu as pltpu
from jax.sharding import PartitionSpec as P

STEPS = 4


def shifted(value, axis, steps):
    count = lax.axis_size(axis)
    pairs = [(source, (source + steps) % count) for source in range(count)]
    return lax.ppermute(value, axis, pairs)


def attend_kernel(table_ref, where_ref, q_ref, *refs, span, group, head_size, steps, scale):
    kv_refs = refs[:steps]
    o_ref = refs[steps]
    s_ref, mx_ref, sm_ref, acc_ref = refs[steps + 1 :]
    cycle = table_ref.shape[0] // 2
    myself = where_ref[1]
    query_span = table_ref[2 * myself + where_ref[0]]
    key_spans = [
        table_ref[2 * ((myself + cycle - b) % cycle) + t] for b in range(steps) for t in range(2)
    ]
    n = group * span

    mx_ref[...] = jnp.full(mx_ref.shape, -jnp.inf, jnp.float32)
    tiles = [(b, t) for b in range(steps) for t in range(2)]

    def score(idx, b, t, masked):
        k = kv_refs[b][0, t * span : (t + 1) * span, :]
        s = jnp.dot(k, q_ref[...], preferred_element_type=jnp.float32) * scale
        if masked:
            key = lax.broadcasted_iota(jnp.int32, (span, n), 0)
            query = lax.broadcasted_iota(jnp.int32, (span, n), 1) % span
            s = jnp.where(key <= query, s, -jnp.inf)
        s_ref[idx] = s
        mx_ref[...] = jnp.maximum(mx_ref[...], jnp.max(s, axis=0, keepdims=True))

    for idx, (b, t) in enumerate(tiles):
        key_span = key_spans[idx]
        pl.when(key_span < query_span)(functools.partial(score, idx, b, t, False))
        if b == 0:
            pl.when(key_span == query_span)(functools.partial(score, idx, b, t, True))

    sm_ref[...] = jnp.zeros(sm_ref.shape, jnp.float32)
    acc_ref[...] = jnp.zeros(acc_ref.shape, jnp.float32)

    def weigh(idx, b, t):
        p = jnp.exp(s_ref[idx] - mx_ref[...])
        sm_ref[...] += jnp.sum(p, axis=0, keepdims=True)
        v = kv_refs[b][1, t * span : (t + 1) * span, :]
        acc_ref[...] += lax.dot_general(
            v, p.astype(jnp.bfloat16), (((0,), (0,)), ((), ())),
            preferred_element_type=jnp.float32,
        )

    for idx, (b, t) in enumerate(tiles):
        key_span = key_spans[idx]
        pl.when(key_span <= query_span)(functools.partial(weigh, idx, b, t))

    result = acc_ref[...] / sm_ref[...]
    for h in range(group):
        o_ref[:, h * head_size : (h + 1) * head_size] = (
            result[:, h * span : (h + 1) * span].T.astype(o_ref.dtype)
        )


def attend_half(table, where, q2, blocks, *, span, group, head_size, first, count, out_cols, out_block0):
    steps = len(blocks)
    width = group * head_size
    kernel = functools.partial(
        attend_kernel,
        span=span,
        group=group,
        head_size=head_size,
        steps=steps,
        scale=1.0 / head_size**0.5,
    )
    q_spec = pl.BlockSpec((None, head_size, group * span), lambda g, tb, w: (w[0], 0, g + first))
    kv_spec = pl.BlockSpec((2, 2 * span, head_size), lambda g, tb, w: (0, 0, g + first))
    o_spec = pl.BlockSpec((span, width), lambda g, tb, w: (0, out_block0(w) + g))
    flops = 4 * span * 2 * span * steps * head_size * group * count
    return pl.pallas_call(
        kernel,
        out_shape=jax.ShapeDtypeStruct((span, out_cols), jnp.bfloat16),
        grid_spec=pltpu.PrefetchScalarGridSpec(
            num_scalar_prefetch=2,
            grid=(count,),
            in_specs=[q_spec] + [kv_spec] * steps,
            out_specs=o_spec,
            scratch_shapes=[
                pltpu.VMEM((2 * steps, span, group * span), jnp.float32),
                pltpu.VMEM((1, group * span), jnp.float32),
                pltpu.VMEM((1, group * span), jnp.float32),
                pltpu.VMEM((head_size, group * span), jnp.float32),
            ],
        ),
        compiler_params=pltpu.CompilerParams(dimension_semantics=("arbitrary",)),
        cost_estimate=pl.CostEstimate(
            flops=flops,
            transcendentals=flops // (4 * head_size),
            bytes_accessed=2 * span * width * count * 2 + steps * 2 * 2 * span * count * head_size * 2,
        ),
    )(table, where, q2, *blocks)


def body(queries, key_value, span_table):
    rows = queries.shape[0]
    heads_here = queries.shape[1]
    head_size = queries.shape[2]
    kv_here = key_value.shape[2]
    group = heads_here // kv_here
    span = rows // 2
    cycle = lax.axis_size("ctx")
    myself = lax.axis_index("ctx")
    half = lax.axis_index("kvh")
    table = span_table.reshape(cycle, 2)

    q2 = (
        queries.reshape(2, span, heads_here, head_size)
        .transpose(0, 3, 2, 1)
        .reshape(2, head_size, heads_here * span)
    )
    own = key_value.reshape(2, rows, kv_here * head_size)
    first = shifted(own, "ctx", 1)
    third = shifted(own, "ctx", 3)
    pairs = [(d, d ^ 1) for d in range(cycle)]
    second = lax.ppermute(jnp.where(myself % 2 == 0, first, third), "ctx", pairs)
    blocks = [own, first, second, third]

    width = heads_here * head_size
    lanes = jnp.arange(2, dtype=jnp.int32)
    sent_where = jnp.where(lanes == 0, 1 - half, myself).astype(jnp.int32)
    kept_where = jnp.where(lanes == 0, half, myself).astype(jnp.int32)
    common = dict(span=span, group=group, head_size=head_size)
    chunks = 2
    per = kv_here // chunks
    arrived = []
    for j in range(chunks):
        sent = attend_half(
            span_table, sent_where, q2, blocks, first=j * per, count=per,
            out_cols=per * group * head_size, out_block0=lambda w: 0, **common,
        )
        arrived.append(shifted(sent, "kvh", 1))
    out = attend_half(
        span_table, kept_where, q2, blocks, first=0, count=kv_here,
        out_cols=2 * width, out_block0=lambda w: w[0] * kv_here, **common,
    )
    for j in range(chunks):
        out = lax.dynamic_update_slice(
            out, arrived[j], (0, (1 - half) * width + j * per * group * head_size)
        )
    return out


def solution(mesh):
    in_specs = (P("ctx", "kvh", None), P(None, "ctx", "kvh", None), P())
    out_specs = P(("ctx", "kvh"), None)
    return jax.shard_map(body, mesh=mesh, in_specs=in_specs, out_specs=out_specs, check_vma=False)
```

```python
import functools

import jax
import jax.numpy as jnp
from jax import lax
from jax.experimental import pallas as pl
from jax.experimental.pallas import tpu as pltpu
from jax.sharding import PartitionSpec as P

STEPS = 4


def shifted(value, axis, steps):
    count = lax.axis_size(axis)
    pairs = [(source, (source + steps) % count) for source in range(count)]
    return lax.ppermute(value, axis, pairs)


def attend_kernel(table_ref, where_ref, q_ref, *refs, span, group, head_size, steps, scale):
    kv_refs = refs[:steps]
    o_ref = refs[steps]
    s_ref, mx_ref, sm_ref, acc_ref, qt_ref = refs[steps + 1 :]
    cycle = table_ref.shape[0] // 2
    myself = where_ref[1]
    query_span = table_ref[2 * myself + where_ref[0]]
    key_spans = [
        table_ref[2 * ((myself + cycle - b) % cycle) + t] for b in range(steps) for t in range(2)
    ]
    n = group * span

    mx_ref[...] = jnp.full(mx_ref.shape, -jnp.inf, jnp.float32)
    qt_ref[...] = q_ref[...].reshape(n, head_size).T
    tiles = [(b, t) for b in range(steps) for t in range(2)]

    def score(idx, b, t, masked):
        k = kv_refs[b][0, t * span : (t + 1) * span, :]
        s = jnp.dot(k, qt_ref[...], preferred_element_type=jnp.float32) * scale
        if masked:
            key = lax.broadcasted_iota(jnp.int32, (span, n), 0)
            query = lax.broadcasted_iota(jnp.int32, (span, n), 1) % span
            s = jnp.where(key <= query, s, -jnp.inf)
        s_ref[idx] = s
        mx_ref[...] = jnp.maximum(mx_ref[...], jnp.max(s, axis=0, keepdims=True))

    for idx, (b, t) in enumerate(tiles):
        key_span = key_spans[idx]
        pl.when(key_span < query_span)(functools.partial(score, idx, b, t, False))
        if b == 0:
            pl.when(key_span == query_span)(functools.partial(score, idx, b, t, True))

    sm_ref[...] = jnp.zeros(sm_ref.shape, jnp.float32)
    acc_ref[...] = jnp.zeros(acc_ref.shape, jnp.float32)

    def weigh(idx, b, t):
        p = jnp.exp(s_ref[idx] - mx_ref[...])
        sm_ref[...] += jnp.sum(p, axis=0, keepdims=True)
        v = kv_refs[b][1, t * span : (t + 1) * span, :]
        acc_ref[...] += jnp.dot(v.T, p.astype(jnp.bfloat16), preferred_element_type=jnp.float32)

    for idx, (b, t) in enumerate(tiles):
        key_span = key_spans[idx]
        pl.when(key_span <= query_span)(functools.partial(weigh, idx, b, t))

    result = acc_ref[...] / sm_ref[...]
    for h in range(group):
        o_ref[:, h * head_size : (h + 1) * head_size] = (
            result[:, h * span : (h + 1) * span].T.astype(o_ref.dtype)
        )


def attend_half(table, where, q2, blocks, *, span, group, head_size, first, count, out_cols, out_block0):
    steps = len(blocks)
    width = group * head_size
    kernel = functools.partial(
        attend_kernel,
        span=span,
        group=group,
        head_size=head_size,
        steps=steps,
        scale=1.0 / head_size**0.5,
    )
    q_spec = pl.BlockSpec((group, span, head_size), lambda g, tb, w: (g + first, w[0], 0))
    kv_spec = pl.BlockSpec((2, 2 * span, head_size), lambda g, tb, w: (0, 0, g + first))
    o_spec = pl.BlockSpec((span, width), lambda g, tb, w: (0, out_block0(w) + g))
    flops = 4 * span * 2 * span * steps * head_size * group * count
    return pl.pallas_call(
        kernel,
        out_shape=jax.ShapeDtypeStruct((span, out_cols), jnp.bfloat16),
        grid_spec=pltpu.PrefetchScalarGridSpec(
            num_scalar_prefetch=2,
            grid=(count,),
            in_specs=[q_spec] + [kv_spec] * steps,
            out_specs=o_spec,
            scratch_shapes=[
                pltpu.VMEM((2 * steps, span, group * span), jnp.float32),
                pltpu.VMEM((1, group * span), jnp.float32),
                pltpu.VMEM((1, group * span), jnp.float32),
                pltpu.VMEM((head_size, group * span), jnp.float32),
                pltpu.VMEM((head_size, group * span), jnp.bfloat16),
            ],
        ),
        compiler_params=pltpu.CompilerParams(dimension_semantics=("arbitrary",)),
        cost_estimate=pl.CostEstimate(
            flops=flops,
            transcendentals=flops // (4 * head_size),
            bytes_accessed=2 * span * width * count * 2 + steps * 2 * 2 * span * count * head_size * 2,
        ),
    )(table, where, q2, *blocks)


def body(queries, key_value, span_table):
    rows = queries.shape[0]
    heads_here = queries.shape[1]
    head_size = queries.shape[2]
    kv_here = key_value.shape[2]
    group = heads_here // kv_here
    span = rows // 2
    cycle = lax.axis_size("ctx")
    myself = lax.axis_index("ctx")
    half = lax.axis_index("kvh")
    table = span_table.reshape(cycle, 2)

    q2 = jnp.transpose(queries, (1, 0, 2))
    own = key_value.reshape(2, rows, kv_here * head_size)
    first = shifted(own, "ctx", 1)
    third = shifted(own, "ctx", 3)
    pairs = [(d, d ^ 1) for d in range(cycle)]
    second = lax.ppermute(jnp.where(myself % 2 == 0, first, third), "ctx", pairs)
    blocks = [own, first, second, third]

    width = heads_here * head_size
    lanes = jnp.arange(2, dtype=jnp.int32)
    sent_where = jnp.where(lanes == 0, 1 - half, myself).astype(jnp.int32)
    kept_where = jnp.where(lanes == 0, half, myself).astype(jnp.int32)
    common = dict(span=span, group=group, head_size=head_size)
    chunks = 2
    per = kv_here // chunks
    arrived = []
    for j in range(chunks):
        sent = attend_half(
            span_table, sent_where, q2, blocks, first=j * per, count=per,
            out_cols=per * group * head_size, out_block0=lambda w: 0, **common,
        )
        arrived.append(shifted(sent, "kvh", 1))
    out = attend_half(
        span_table, kept_where, q2, blocks, first=0, count=kv_here,
        out_cols=2 * width, out_block0=lambda w: w[0] * kv_here, **common,
    )
    for j in range(chunks):
        out = lax.dynamic_update_slice(
            out, arrived[j], (0, (1 - half) * width + j * per * group * head_size)
        )
    return out


def solution(mesh):
    in_specs = (P("ctx", "kvh", None), P(None, "ctx", "kvh", None), P())
    out_specs = P(("ctx", "kvh"), None)
    return jax.shard_map(body, mesh=mesh, in_specs=in_specs, out_specs=out_specs, check_vma=False)
```

```python
import functools

import jax
import jax.numpy as jnp
from jax import lax
from jax.experimental import pallas as pl
from jax.experimental.pallas import tpu as pltpu
from jax.sharding import PartitionSpec as P

STEPS = 4


def shifted(value, axis, steps):
    count = lax.axis_size(axis)
    pairs = [(source, (source + steps) % count) for source in range(count)]
    return lax.ppermute(value, axis, pairs)


def attend_kernel(table_ref, where_ref, q_ref, *refs, span, group, head_size, steps, scale):
    kv_refs = refs[:steps]
    o_ref = refs[steps]
    mx_ref, sm_ref, acc_ref = refs[steps + 1 :]
    cycle = table_ref.shape[0] // 2
    myself = where_ref[1]
    query_span = table_ref[2 * myself + where_ref[0]]
    key_spans = [
        table_ref[2 * ((myself + cycle - b) % cycle) + t] for b in range(steps) for t in range(2)
    ]
    n = group * span

    tiles = [(b, t) for b in range(steps) for t in range(2)]
    row = lax.broadcasted_iota(jnp.int32, (n, span), 0) % span
    col = lax.broadcasted_iota(jnp.int32, (n, span), 1)

    def scores(idx, b, t):
        k = kv_refs[b][0, t * span : (t + 1) * span, :]
        q = q_ref[...].reshape(n, head_size)
        s = lax.dot_general(
            q, k, (((1,), (1,)), ((), ())), preferred_element_type=jnp.float32
        ) * scale
        if b == 0:
            s = jnp.where((col <= row) | (key_spans[idx] < query_span), s, -jnp.inf)
        return s

    mx_ref[...] = scores(0, 0, 0)

    def widen(idx, b, t):
        mx_ref[...] = jnp.maximum(mx_ref[...], scores(idx, b, t))

    for idx, (b, t) in enumerate(tiles[1:], start=1):
        pl.when(key_spans[idx] <= query_span)(functools.partial(widen, idx, b, t))

    m = jnp.max(mx_ref[...], axis=1, keepdims=True)
    mx_ref[...] = jnp.broadcast_to(m, (n, span))

    def weigh(idx, b, t, first):
        p = jnp.exp(scores(idx, b, t) - mx_ref[...])
        v = kv_refs[b][1, t * span : (t + 1) * span, :]
        out = jnp.dot(p.astype(jnp.bfloat16), v, preferred_element_type=jnp.float32)
        if first:
            sm_ref[...] = p
            acc_ref[...] = out
        else:
            sm_ref[...] += p
            acc_ref[...] += out

    weigh(0, 0, 0, True)
    for idx, (b, t) in enumerate(tiles[1:], start=1):
        pl.when(key_spans[idx] <= query_span)(functools.partial(weigh, idx, b, t, False))

    total = jnp.sum(sm_ref[...], axis=1, keepdims=True)
    result = acc_ref[...] / total
    for h in range(group):
        o_ref[:, h * head_size : (h + 1) * head_size] = result[
            h * span : (h + 1) * span, :
        ].astype(o_ref.dtype)


def attend_half(table, where, q2, blocks, *, span, group, head_size, first, count, out_cols, out_block0):
    steps = len(blocks)
    width = group * head_size
    kernel = functools.partial(
        attend_kernel,
        span=span,
        group=group,
        head_size=head_size,
        steps=steps,
        scale=1.0 / head_size**0.5,
    )
    q_spec = pl.BlockSpec((group, span, head_size), lambda g, tb, w: (g + first, w[0], 0))
    kv_spec = pl.BlockSpec((2, 2 * span, head_size), lambda g, tb, w: (0, 0, g + first))
    o_spec = pl.BlockSpec((span, width), lambda g, tb, w: (0, out_block0(w) + g))
    flops = 4 * span * 2 * span * steps * head_size * group * count
    return pl.pallas_call(
        kernel,
        out_shape=jax.ShapeDtypeStruct((span, out_cols), jnp.bfloat16),
        grid_spec=pltpu.PrefetchScalarGridSpec(
            num_scalar_prefetch=2,
            grid=(count,),
            in_specs=[q_spec] + [kv_spec] * steps,
            out_specs=o_spec,
            scratch_shapes=[
                pltpu.VMEM((group * span, span), jnp.float32),
                pltpu.VMEM((group * span, span), jnp.float32),
                pltpu.VMEM((group * span, head_size), jnp.float32),
            ],
        ),
        compiler_params=pltpu.CompilerParams(dimension_semantics=("arbitrary",)),
        cost_estimate=pl.CostEstimate(
            flops=flops,
            transcendentals=flops // (4 * head_size),
            bytes_accessed=2 * span * width * count * 2 + steps * 2 * 2 * span * count * head_size * 2,
        ),
    )(table, where, q2, *blocks)


def body(queries, key_value, span_table):
    rows = queries.shape[0]
    heads_here = queries.shape[1]
    head_size = queries.shape[2]
    kv_here = key_value.shape[2]
    group = heads_here // kv_here
    span = rows // 2
    cycle = lax.axis_size("ctx")
    myself = lax.axis_index("ctx")
    half = lax.axis_index("kvh")
    table = span_table.reshape(cycle, 2)

    q2 = jnp.transpose(queries, (1, 0, 2))
    own = key_value.reshape(2, rows, kv_here * head_size)
    first = shifted(own, "ctx", 1)
    third = shifted(own, "ctx", 3)
    pairs = [(d, d ^ 1) for d in range(cycle)]
    second = lax.ppermute(jnp.where(myself % 2 == 0, first, third), "ctx", pairs)
    blocks = [own, first, second, third]

    width = heads_here * head_size
    lanes = jnp.arange(2, dtype=jnp.int32)
    sent_where = jnp.where(lanes == 0, 1 - half, myself).astype(jnp.int32)
    kept_where = jnp.where(lanes == 0, half, myself).astype(jnp.int32)
    common = dict(span=span, group=group, head_size=head_size)
    chunks = 2
    per = kv_here // chunks
    arrived = []
    for j in range(chunks):
        sent = attend_half(
            span_table, sent_where, q2, blocks, first=j * per, count=per,
            out_cols=per * group * head_size, out_block0=lambda w: 0, **common,
        )
        arrived.append(shifted(sent, "kvh", 1))
    out = attend_half(
        span_table, kept_where, q2, blocks, first=0, count=kv_here,
        out_cols=2 * width, out_block0=lambda w: w[0] * kv_here, **common,
    )
    for j in range(chunks):
        out = lax.dynamic_update_slice(
            out, arrived[j], (0, (1 - half) * width + j * per * group * head_size)
        )
    return out


def solution(mesh):
    in_specs = (P("ctx", "kvh", None), P(None, "ctx", "kvh", None), P())
    out_specs = P(("ctx", "kvh"), None)
    return jax.shard_map(body, mesh=mesh, in_specs=in_specs, out_specs=out_specs, check_vma=False)
```

```python
import functools

import jax
import jax.numpy as jnp
from jax import lax
from jax.experimental import pallas as pl
from jax.experimental.pallas import tpu as pltpu
from jax.sharding import PartitionSpec as P

STEPS = 4


def shifted(value, axis, steps):
    count = lax.axis_size(axis)
    pairs = [(source, (source + steps) % count) for source in range(count)]
    return lax.ppermute(value, axis, pairs)


def attend_kernel(table_ref, where_ref, q_ref, *refs, span, group, head_size, steps, scale):
    kv_refs = refs[:steps]
    o_ref = refs[steps]
    s_ref, mx_ref, sm_ref, acc_ref = refs[steps + 1 :]
    cycle = table_ref.shape[0] // 2
    myself = where_ref[1]
    query_span = table_ref[2 * myself + where_ref[0]]
    key_spans = [
        table_ref[2 * ((myself + cycle - b) % cycle) + t] for b in range(steps) for t in range(2)
    ]
    n = group * span

    tiles = [(b, t) for b in range(steps) for t in range(2)]

    def score(idx, b, t, first):
        k = kv_refs[b][0, t * span : (t + 1) * span, :]
        q = q_ref[...].reshape(n, head_size)
        s = jnp.dot(q, k.T, preferred_element_type=jnp.float32) * scale
        if b == 0:
            row = lax.broadcasted_iota(jnp.int32, (n, span), 0) % span
            col = lax.broadcasted_iota(jnp.int32, (n, span), 1)
            s = jnp.where((col <= row) | (key_spans[idx] < query_span), s, -jnp.inf)
        s_ref[idx] = s
        if first:
            mx_ref[...] = s
        else:
            mx_ref[...] = jnp.maximum(mx_ref[...], s)

    score(0, 0, 0, True)
    for idx, (b, t) in enumerate(tiles[1:], start=1):
        pl.when(key_spans[idx] <= query_span)(functools.partial(score, idx, b, t, False))

    m = jnp.max(mx_ref[...], axis=1, keepdims=True)
    mx_ref[...] = jnp.broadcast_to(m, (n, span))

    def weigh(idx, b, t, first):
        p = jnp.exp(s_ref[idx] - mx_ref[...])
        v = kv_refs[b][1, t * span : (t + 1) * span, :]
        out = jnp.dot(p.astype(jnp.bfloat16), v, preferred_element_type=jnp.float32)
        if first:
            sm_ref[...] = p
            acc_ref[...] = out
        else:
            sm_ref[...] += p
            acc_ref[...] += out

    weigh(0, 0, 0, True)
    for idx, (b, t) in enumerate(tiles[1:], start=1):
        pl.when(key_spans[idx] <= query_span)(functools.partial(weigh, idx, b, t, False))

    total = jnp.sum(sm_ref[...], axis=1, keepdims=True)
    result = acc_ref[...] / total
    for h in range(group):
        o_ref[:, h * head_size : (h + 1) * head_size] = result[
            h * span : (h + 1) * span, :
        ].astype(o_ref.dtype)


def attend_half(table, where, q2, blocks, *, span, group, head_size, first, count, out_cols, out_block0):
    steps = len(blocks)
    width = group * head_size
    kernel = functools.partial(
        attend_kernel,
        span=span,
        group=group,
        head_size=head_size,
        steps=steps,
        scale=1.0 / head_size**0.5,
    )
    q_spec = pl.BlockSpec((group, span, head_size), lambda g, tb, w: (g + first, w[0], 0))
    kv_spec = pl.BlockSpec((2, 2 * span, head_size), lambda g, tb, w: (0, 0, g + first))
    o_spec = pl.BlockSpec((span, width), lambda g, tb, w: (0, out_block0(w) + g))
    flops = 4 * span * 2 * span * steps * head_size * group * count
    return pl.pallas_call(
        kernel,
        out_shape=jax.ShapeDtypeStruct((span, out_cols), jnp.bfloat16),
        grid_spec=pltpu.PrefetchScalarGridSpec(
            num_scalar_prefetch=2,
            grid=(count,),
            in_specs=[q_spec] + [kv_spec] * steps,
            out_specs=o_spec,
            scratch_shapes=[
                pltpu.VMEM((2 * steps, group * span, span), jnp.float32),
                pltpu.VMEM((group * span, span), jnp.float32),
                pltpu.VMEM((group * span, span), jnp.float32),
                pltpu.VMEM((group * span, head_size), jnp.float32),
            ],
        ),
        compiler_params=pltpu.CompilerParams(dimension_semantics=("arbitrary",)),
        cost_estimate=pl.CostEstimate(
            flops=flops,
            transcendentals=flops // (4 * head_size),
            bytes_accessed=2 * span * width * count * 2 + steps * 2 * 2 * span * count * head_size * 2,
        ),
    )(table, where, q2, *blocks)


def body(queries, key_value, span_table):
    rows = queries.shape[0]
    heads_here = queries.shape[1]
    head_size = queries.shape[2]
    kv_here = key_value.shape[2]
    group = heads_here // kv_here
    span = rows // 2
    cycle = lax.axis_size("ctx")
    myself = lax.axis_index("ctx")
    half = lax.axis_index("kvh")
    table = span_table.reshape(cycle, 2)

    q2 = jnp.transpose(queries, (1, 0, 2))
    own = key_value.reshape(2, rows, kv_here * head_size)
    first = shifted(own, "ctx", 1)
    third = shifted(own, "ctx", 3)
    pairs = [(d, d ^ 1) for d in range(cycle)]
    second = lax.ppermute(jnp.where(myself % 2 == 0, first, third), "ctx", pairs)
    blocks = [own, first, second, third]

    width = heads_here * head_size
    lanes = jnp.arange(2, dtype=jnp.int32)
    sent_where = jnp.where(lanes == 0, 1 - half, myself).astype(jnp.int32)
    kept_where = jnp.where(lanes == 0, half, myself).astype(jnp.int32)
    common = dict(span=span, group=group, head_size=head_size)
    chunks = 2
    per = kv_here // chunks
    arrived = []
    for j in range(chunks):
        sent = attend_half(
            span_table, sent_where, q2, blocks, first=j * per, count=per,
            out_cols=per * group * head_size, out_block0=lambda w: 0, **common,
        )
        arrived.append(shifted(sent, "kvh", 1))
    out = attend_half(
        span_table, kept_where, q2, blocks, first=0, count=kv_here,
        out_cols=2 * width, out_block0=lambda w: w[0] * kv_here, **common,
    )
    for j in range(chunks):
        out = lax.dynamic_update_slice(
            out, arrived[j], (0, (1 - half) * width + j * per * group * head_size)
        )
    return out


def solution(mesh):
    in_specs = (P("ctx", "kvh", None), P(None, "ctx", "kvh", None), P())
    out_specs = P(("ctx", "kvh"), None)
    return jax.shard_map(body, mesh=mesh, in_specs=in_specs, out_specs=out_specs, check_vma=False)
```

```python
import functools

import jax
import jax.numpy as jnp
from jax import lax
from jax.experimental import pallas as pl
from jax.experimental.pallas import tpu as pltpu
from jax.sharding import PartitionSpec as P

STEPS = 4


def shifted(value, axis, steps):
    count = lax.axis_size(axis)
    pairs = [(source, (source + steps) % count) for source in range(count)]
    return lax.ppermute(value, axis, pairs)


def attend_kernel(table_ref, where_ref, q_ref, *refs, span, group, head_size, steps, scale):
    kv_refs = refs[:steps]
    o_ref = refs[steps]
    s_ref, mx_ref, sm_ref, acc_ref = refs[steps + 1 :]
    cycle = table_ref.shape[0] // 2
    myself = where_ref[1]
    query_span = table_ref[2 * myself + where_ref[0]]
    key_spans = [
        table_ref[2 * ((myself + cycle - b) % cycle) + t] for b in range(steps) for t in range(2)
    ]
    n = group * span

    tiles = [(b, t) for b in range(steps) for t in range(2)]

    def score(idx, b, t, first):
        k = kv_refs[b][0, t * span : (t + 1) * span, :]
        q = q_ref[...].reshape(n, head_size)
        s = jnp.dot(q, k.T, preferred_element_type=jnp.float32) * scale
        if b == 0:
            row = lax.broadcasted_iota(jnp.int32, (n, span), 0) % span
            col = lax.broadcasted_iota(jnp.int32, (n, span), 1)
            s = jnp.where((col <= row) | (key_spans[idx] < query_span), s, -jnp.inf)
        s_ref[idx] = s
        if first:
            mx_ref[...] = s
        else:
            mx_ref[...] = jnp.maximum(mx_ref[...], s)

    score(0, 0, 0, True)
    for idx, (b, t) in enumerate(tiles[1:], start=1):
        pl.when(key_spans[idx] <= query_span)(functools.partial(score, idx, b, t, False))

    m = jnp.max(mx_ref[...], axis=1, keepdims=True)
    mx_ref[...] = jnp.broadcast_to(m, (n, span))

    def weigh(idx, b, t, first):
        p = jnp.exp(s_ref[idx] - mx_ref[...])
        v = kv_refs[b][1, t * span : (t + 1) * span, :]
        out = jnp.dot(p.astype(jnp.bfloat16), v, preferred_element_type=jnp.float32)
        if first:
            sm_ref[...] = p
            acc_ref[...] = out
        else:
            sm_ref[...] += p
            acc_ref[...] += out

    weigh(0, 0, 0, True)
    for idx, (b, t) in enumerate(tiles[1:], start=1):
        pl.when(key_spans[idx] <= query_span)(functools.partial(weigh, idx, b, t, False))

    total = jnp.sum(sm_ref[...], axis=1, keepdims=True)
    result = acc_ref[...] / total
    for h in range(group):
        o_ref[:, h * head_size : (h + 1) * head_size] = result[
            h * span : (h + 1) * span, :
        ].astype(o_ref.dtype)


def attend_half(table, where, q2, blocks, *, span, group, head_size, first, count, out_cols, out_block0):
    steps = len(blocks)
    width = group * head_size
    kernel = functools.partial(
        attend_kernel,
        span=span,
        group=group,
        head_size=head_size,
        steps=steps,
        scale=1.0 / head_size**0.5,
    )
    q_spec = pl.BlockSpec((group, span, head_size), lambda g, tb, w: (g + first, w[0], 0))
    kv_spec = pl.BlockSpec((2, 2 * span, head_size), lambda g, tb, w: (0, 0, g + first))
    o_spec = pl.BlockSpec((span, width), lambda g, tb, w: (0, out_block0(w) + g))
    flops = 4 * span * 2 * span * steps * head_size * group * count
    return pl.pallas_call(
        kernel,
        out_shape=jax.ShapeDtypeStruct((span, out_cols), jnp.bfloat16),
        grid_spec=pltpu.PrefetchScalarGridSpec(
            num_scalar_prefetch=2,
            grid=(count,),
            in_specs=[q_spec] + [kv_spec] * steps,
            out_specs=o_spec,
            scratch_shapes=[
                pltpu.VMEM((2 * steps, group * span, span), jnp.float32),
                pltpu.VMEM((group * span, span), jnp.float32),
                pltpu.VMEM((group * span, span), jnp.float32),
                pltpu.VMEM((group * span, head_size), jnp.float32),
            ],
        ),
        compiler_params=pltpu.CompilerParams(dimension_semantics=("arbitrary",)),
        cost_estimate=pl.CostEstimate(
            flops=flops,
            transcendentals=flops // (4 * head_size),
            bytes_accessed=2 * span * width * count * 2 + steps * 2 * 2 * span * count * head_size * 2,
        ),
    )(table, where, q2, *blocks)


def body(queries, key_value, span_table):
    rows = queries.shape[0]
    heads_here = queries.shape[1]
    head_size = queries.shape[2]
    kv_here = key_value.shape[2]
    group = heads_here // kv_here
    span = rows // 2
    cycle = lax.axis_size("ctx")
    myself = lax.axis_index("ctx")
    half = lax.axis_index("kvh")
    table = span_table.reshape(cycle, 2)

    q2 = jnp.transpose(queries, (1, 0, 2))
    own = key_value.reshape(2, rows, kv_here * head_size)
    first = shifted(own, "ctx", 1)
    third = shifted(own, "ctx", 3)
    first, third, q2 = lax.optimization_barrier((first, third, q2))
    pairs = [(d, d ^ 1) for d in range(cycle)]
    second = lax.ppermute(jnp.where(myself % 2 == 0, first, third), "ctx", pairs)
    blocks = [own, first, second, third]

    width = heads_here * head_size
    lanes = jnp.arange(2, dtype=jnp.int32)
    sent_where = jnp.where(lanes == 0, 1 - half, myself).astype(jnp.int32)
    kept_where = jnp.where(lanes == 0, half, myself).astype(jnp.int32)
    common = dict(span=span, group=group, head_size=head_size)
    chunks = 2
    per = kv_here // chunks
    arrived = []
    for j in range(chunks):
        sent = attend_half(
            span_table, sent_where, q2, blocks, first=j * per, count=per,
            out_cols=per * group * head_size, out_block0=lambda w: 0, **common,
        )
        arrived.append(shifted(sent, "kvh", 1))
    out = attend_half(
        span_table, kept_where, q2, blocks, first=0, count=kv_here,
        out_cols=2 * width, out_block0=lambda w: w[0] * kv_here, **common,
    )
    for j in range(chunks):
        out = lax.dynamic_update_slice(
            out, arrived[j], (0, (1 - half) * width + j * per * group * head_size)
        )
    return out


def solution(mesh):
    in_specs = (P("ctx", "kvh", None), P(None, "ctx", "kvh", None), P())
    out_specs = P(("ctx", "kvh"), None)
    return jax.shard_map(body, mesh=mesh, in_specs=in_specs, out_specs=out_specs, check_vma=False)
```

```python
import functools

import jax
import jax.numpy as jnp
from jax import lax
from jax.experimental import pallas as pl
from jax.experimental.pallas import tpu as pltpu
from jax.sharding import PartitionSpec as P

STEPS = 4


def shifted(value, axis, steps):
    count = lax.axis_size(axis)
    pairs = [(source, (source + steps) % count) for source in range(count)]
    return lax.ppermute(value, axis, pairs)


def attend_kernel(table_ref, where_ref, q_ref, *refs, span, group, head_size, steps, scale):
    kv_refs = refs[:steps]
    o_ref = refs[steps]
    s_ref, mx_ref, sm_ref, acc_ref = refs[steps + 1 :]
    cycle = table_ref.shape[0] // 2
    myself = where_ref[1]
    query_span = table_ref[2 * myself + where_ref[0]]
    key_spans = [
        table_ref[2 * ((myself + cycle - b) % cycle) + t] for b in range(steps) for t in range(2)
    ]
    n = group * span

    tiles = [(b, t) for b in range(steps) for t in range(2)]

    def score(idx, b, t, first):
        k = kv_refs[b][0, t * span : (t + 1) * span, :]
        q = q_ref[...].reshape(n, head_size)
        s = jnp.dot(q, k.T, preferred_element_type=jnp.float32) * scale
        if b == 0:
            row = lax.broadcasted_iota(jnp.int32, (n, span), 0) % span
            col = lax.broadcasted_iota(jnp.int32, (n, span), 1)
            s = jnp.where((col <= row) | (key_spans[idx] < query_span), s, -jnp.inf)
        s_ref[idx] = s
        if first:
            mx_ref[...] = s
        else:
            mx_ref[...] = jnp.maximum(mx_ref[...], s)

    score(0, 0, 0, True)
    for idx, (b, t) in enumerate(tiles[1:], start=1):
        pl.when(key_spans[idx] <= query_span)(functools.partial(score, idx, b, t, False))

    m = jnp.max(mx_ref[...], axis=1, keepdims=True)
    mx_ref[...] = jnp.broadcast_to(m, (n, span))

    def weigh(idx, b, t, first):
        p = jnp.exp(s_ref[idx] - mx_ref[...])
        v = kv_refs[b][1, t * span : (t + 1) * span, :]
        out = jnp.dot(p.astype(jnp.bfloat16), v, preferred_element_type=jnp.float32)
        if first:
            sm_ref[...] = p
            acc_ref[...] = out
        else:
            sm_ref[...] += p
            acc_ref[...] += out

    weigh(0, 0, 0, True)
    for idx, (b, t) in enumerate(tiles[1:], start=1):
        pl.when(key_spans[idx] <= query_span)(functools.partial(weigh, idx, b, t, False))

    total = jnp.sum(sm_ref[...], axis=1, keepdims=True)
    result = acc_ref[...] / total
    for h in range(group):
        o_ref[:, h * head_size : (h + 1) * head_size] = result[
            h * span : (h + 1) * span, :
        ].astype(o_ref.dtype)


def attend_half(table, where, q2, blocks, *, span, group, head_size, first, count, out_cols, out_block0):
    steps = len(blocks)
    width = group * head_size
    kernel = functools.partial(
        attend_kernel,
        span=span,
        group=group,
        head_size=head_size,
        steps=steps,
        scale=1.0 / head_size**0.5,
    )
    q_spec = pl.BlockSpec((group, span, head_size), lambda g, tb, w: (g + first, w[0], 0))
    kv_spec = pl.BlockSpec((2, 2 * span, head_size), lambda g, tb, w: (0, 0, g + first))
    o_spec = pl.BlockSpec((span, width), lambda g, tb, w: (0, out_block0(w) + g))
    flops = 4 * span * 2 * span * steps * head_size * group * count
    return pl.pallas_call(
        kernel,
        out_shape=jax.ShapeDtypeStruct((span, out_cols), jnp.bfloat16),
        grid_spec=pltpu.PrefetchScalarGridSpec(
            num_scalar_prefetch=2,
            grid=(count,),
            in_specs=[q_spec] + [kv_spec] * steps,
            out_specs=o_spec,
            scratch_shapes=[
                pltpu.VMEM((2 * steps, group * span, span), jnp.float32),
                pltpu.VMEM((group * span, span), jnp.float32),
                pltpu.VMEM((group * span, span), jnp.float32),
                pltpu.VMEM((group * span, head_size), jnp.float32),
            ],
        ),
        compiler_params=pltpu.CompilerParams(dimension_semantics=("arbitrary",)),
        cost_estimate=pl.CostEstimate(
            flops=flops,
            transcendentals=flops // (4 * head_size),
            bytes_accessed=2 * span * width * count * 2 + steps * 2 * 2 * span * count * head_size * 2,
        ),
    )(table, where, q2, *blocks)


def body(queries, key_value, span_table):
    rows = queries.shape[0]
    heads_here = queries.shape[1]
    head_size = queries.shape[2]
    kv_here = key_value.shape[2]
    group = heads_here // kv_here
    span = rows // 2
    cycle = lax.axis_size("ctx")
    myself = lax.axis_index("ctx")
    half = lax.axis_index("kvh")
    table = span_table.reshape(cycle, 2)

    q2 = jnp.transpose(queries, (1, 0, 2))
    own = key_value.reshape(2, rows, kv_here * head_size)
    first = shifted(own, "ctx", 1)
    third = shifted(own, "ctx", 3)

    width = heads_here * head_size
    lanes = jnp.arange(2, dtype=jnp.int32)
    sent_where = jnp.where(lanes == 0, 1 - half, myself).astype(jnp.int32)
    kept_where = jnp.where(lanes == 0, half, myself).astype(jnp.int32)
    first, third, q2, sent_where, kept_where = lax.optimization_barrier(
        (first, third, q2, sent_where, kept_where)
    )
    pairs = [(d, d ^ 1) for d in range(cycle)]
    second = lax.ppermute(jnp.where(myself % 2 == 0, first, third), "ctx", pairs)
    blocks = [own, first, second, third]
    common = dict(span=span, group=group, head_size=head_size)
    chunks = 2
    per = kv_here // chunks
    arrived = []
    for j in range(chunks):
        sent = attend_half(
            span_table, sent_where, q2, blocks, first=j * per, count=per,
            out_cols=per * group * head_size, out_block0=lambda w: 0, **common,
        )
        arrived.append(shifted(sent, "kvh", 1))
    out = attend_half(
        span_table, kept_where, q2, blocks, first=0, count=kv_here,
        out_cols=2 * width, out_block0=lambda w: w[0] * kv_here, **common,
    )
    for j in range(chunks):
        out = lax.dynamic_update_slice(
            out, arrived[j], (0, (1 - half) * width + j * per * group * head_size)
        )
    return out


def solution(mesh):
    in_specs = (P("ctx", "kvh", None), P(None, "ctx", "kvh", None), P())
    out_specs = P(("ctx", "kvh"), None)
    return jax.shard_map(body, mesh=mesh, in_specs=in_specs, out_specs=out_specs, check_vma=False)
```

```python
import functools

import jax
import jax.numpy as jnp
from jax import lax
from jax.experimental import pallas as pl
from jax.experimental.pallas import tpu as pltpu
from jax.sharding import PartitionSpec as P

STEPS = 4


def shifted(value, axis, steps):
    count = lax.axis_size(axis)
    pairs = [(source, (source + steps) % count) for source in range(count)]
    return lax.ppermute(value, axis, pairs)


def attend_kernel(table_ref, where_ref, q_ref, *refs, span, group, head_size, steps, scale):
    kv_refs = refs[:steps]
    o_ref = refs[steps]
    s_ref, mx_ref, sm_ref, p_ref, v_ref = refs[steps + 1 :]
    cycle = table_ref.shape[0] // 2
    half = where_ref[0]
    myself = where_ref[1]
    query_span = table_ref[2 * myself + half]
    n = group * span

    def key_span(b, t):
        return table_ref[2 * ((myself + cycle - b) % cycle) + t]

    def run(tiles, always, diag):
        def score(idx, b, t, first):
            k = kv_refs[b][0, t * span : (t + 1) * span, :]
            q = q_ref[...].reshape(n, head_size)
            s = jnp.dot(q, k.T, preferred_element_type=jnp.float32) * scale
            if idx == diag:
                row = lax.broadcasted_iota(jnp.int32, (n, span), 0) % span
                col = lax.broadcasted_iota(jnp.int32, (n, span), 1)
                s = jnp.where(col <= row, s, -jnp.inf)
            s_ref[idx] = s
            if first:
                mx_ref[...] = s
            else:
                mx_ref[...] = jnp.maximum(mx_ref[...], s)

        def weigh(idx, first):
            p = jnp.exp(s_ref[idx] - mx_ref[...])
            p_ref[:, idx * span : (idx + 1) * span] = p.astype(jnp.bfloat16)
            if first:
                sm_ref[...] = p
            else:
                sm_ref[...] += p

        def hide(idx):
            p_ref[:, idx * span : (idx + 1) * span] = jnp.zeros((n, span), jnp.bfloat16)

        score(0, *tiles[0], True)
        for idx, (b, t) in enumerate(tiles[1:], start=1):
            if always[idx]:
                score(idx, b, t, False)
            else:
                pl.when(key_span(b, t) < query_span)(functools.partial(score, idx, b, t, False))

        m = jnp.max(mx_ref[...], axis=1, keepdims=True)
        mx_ref[...] = jnp.broadcast_to(m, (n, span))

        weigh(0, True)
        for idx, (b, t) in enumerate(tiles[1:], start=1):
            if always[idx]:
                weigh(idx, False)
            else:
                visible = key_span(b, t) < query_span
                pl.when(visible)(functools.partial(weigh, idx, False))
                pl.when(jnp.logical_not(visible))(functools.partial(hide, idx))
        for idx, (b, t) in enumerate(tiles):
            v_ref[idx * span : (idx + 1) * span, :] = kv_refs[b][1, t * span : (t + 1) * span, :]
        width = len(tiles) * span
        acc = jnp.dot(p_ref[:, :width], v_ref[:width, :], preferred_element_type=jnp.float32)
        total = jnp.sum(sm_ref[...], axis=1, keepdims=True)
        result = acc / total
        for h in range(group):
            o_ref[:, h * head_size : (h + 1) * head_size] = result[
                h * span : (h + 1) * span, :
            ].astype(o_ref.dtype)

    early = [(b, 0) for b in range(steps)]
    late = early + [(b, 1) for b in range(steps)]
    pl.when(half == 0)(lambda: run(early, [b == 0 for b, t in early], 0))
    pl.when(half == 1)(lambda: run(late, [t == 0 or b == 0 for b, t in late], steps))


def attend_half(table, where, q2, blocks, *, span, group, head_size, first, count, out_cols, out_block0):
    steps = len(blocks)
    width = group * head_size
    kernel = functools.partial(
        attend_kernel,
        span=span,
        group=group,
        head_size=head_size,
        steps=steps,
        scale=1.0 / head_size**0.5,
    )
    q_spec = pl.BlockSpec((group, span, head_size), lambda g, tb, w: (g + first, w[0], 0))
    kv_spec = pl.BlockSpec((2, 2 * span, head_size), lambda g, tb, w: (0, 0, g + first))
    o_spec = pl.BlockSpec((span, width), lambda g, tb, w: (0, out_block0(w) + g))
    flops = 4 * span * 2 * span * steps * head_size * group * count
    return pl.pallas_call(
        kernel,
        out_shape=jax.ShapeDtypeStruct((span, out_cols), jnp.bfloat16),
        grid_spec=pltpu.PrefetchScalarGridSpec(
            num_scalar_prefetch=2,
            grid=(count,),
            in_specs=[q_spec] + [kv_spec] * steps,
            out_specs=o_spec,
            scratch_shapes=[
                pltpu.VMEM((2 * steps, group * span, span), jnp.float32),
                pltpu.VMEM((group * span, span), jnp.float32),
                pltpu.VMEM((group * span, span), jnp.float32),
                pltpu.VMEM((group * span, 2 * steps * span), jnp.bfloat16),
                pltpu.VMEM((2 * steps * span, head_size), jnp.bfloat16),
            ],
        ),
        compiler_params=pltpu.CompilerParams(dimension_semantics=("arbitrary",)),
        cost_estimate=pl.CostEstimate(
            flops=flops,
            transcendentals=flops // (4 * head_size),
            bytes_accessed=2 * span * width * count * 2 + steps * 2 * 2 * span * count * head_size * 2,
        ),
    )(table, where, q2, *blocks)


def body(queries, key_value, span_table):
    rows = queries.shape[0]
    heads_here = queries.shape[1]
    head_size = queries.shape[2]
    kv_here = key_value.shape[2]
    group = heads_here // kv_here
    span = rows // 2
    cycle = lax.axis_size("ctx")
    myself = lax.axis_index("ctx")
    half = lax.axis_index("kvh")
    table = span_table.reshape(cycle, 2)

    q2 = jnp.transpose(queries, (1, 0, 2))
    own = key_value.reshape(2, rows, kv_here * head_size)
    first = shifted(own, "ctx", 1)
    third = shifted(own, "ctx", 3)
    pairs = [(d, d ^ 1) for d in range(cycle)]
    second = lax.ppermute(jnp.where(myself % 2 == 0, first, third), "ctx", pairs)
    blocks = [own, first, second, third]

    width = heads_here * head_size
    lanes = jnp.arange(2, dtype=jnp.int32)
    sent_where = jnp.where(lanes == 0, 1 - half, myself).astype(jnp.int32)
    kept_where = jnp.where(lanes == 0, half, myself).astype(jnp.int32)
    common = dict(span=span, group=group, head_size=head_size)
    chunks = 2
    per = kv_here // chunks
    arrived = []
    for j in range(chunks):
        sent = attend_half(
            span_table, sent_where, q2, blocks, first=j * per, count=per,
            out_cols=per * group * head_size, out_block0=lambda w: 0, **common,
        )
        arrived.append(shifted(sent, "kvh", 1))
    out = attend_half(
        span_table, kept_where, q2, blocks, first=0, count=kv_here,
        out_cols=2 * width, out_block0=lambda w: w[0] * kv_here, **common,
    )
    for j in range(chunks):
        out = lax.dynamic_update_slice(
            out, arrived[j], (0, (1 - half) * width + j * per * group * head_size)
        )
    return out


def solution(mesh):
    in_specs = (P("ctx", "kvh", None), P(None, "ctx", "kvh", None), P())
    out_specs = P(("ctx", "kvh"), None)
    return jax.shard_map(body, mesh=mesh, in_specs=in_specs, out_specs=out_specs, check_vma=False)
```

```python
import functools

import jax
import jax.numpy as jnp
from jax import lax
from jax.experimental import pallas as pl
from jax.experimental.pallas import tpu as pltpu
from jax.sharding import PartitionSpec as P

STEPS = 4


def shifted(value, axis, steps):
    count = lax.axis_size(axis)
    pairs = [(source, (source + steps) % count) for source in range(count)]
    return lax.ppermute(value, axis, pairs)


def attend_kernel(table_ref, where_ref, q_ref, *refs, span, group, head_size, steps, scale):
    kv_refs = refs[:steps]
    o_ref = refs[steps]
    s_ref, mx_ref, sm_ref, p_ref, v_ref = refs[steps + 1 :]
    cycle = table_ref.shape[0] // 2
    half = where_ref[0]
    myself = where_ref[1]
    query_span = table_ref[2 * myself + half]
    n = group * span

    def key_span(b, t):
        return table_ref[2 * ((myself + cycle - b) % cycle) + t]

    def run(tiles, always, diag):
        def score(idx, b, t, first):
            k = kv_refs[b][0, t * span : (t + 1) * span, :]
            q = q_ref[...].reshape(n, head_size)
            s = jnp.dot(q, k.T, preferred_element_type=jnp.float32) * scale
            if idx == diag:
                row = lax.broadcasted_iota(jnp.int32, (n, span), 0) % span
                col = lax.broadcasted_iota(jnp.int32, (n, span), 1)
                s = jnp.where(col <= row, s, -jnp.inf)
            s_ref[idx] = s
            if first:
                mx_ref[...] = s
            else:
                mx_ref[...] = jnp.maximum(mx_ref[...], s)

        def weigh(idx, first):
            p = jnp.exp(s_ref[idx] - mx_ref[...])
            p_ref[:, idx * span : (idx + 1) * span] = p.astype(jnp.bfloat16)
            if first:
                sm_ref[...] = p
            else:
                sm_ref[...] += p

        def hide(idx):
            p_ref[:, idx * span : (idx + 1) * span] = jnp.zeros((n, span), jnp.bfloat16)

        score(0, *tiles[0], True)
        for idx, (b, t) in enumerate(tiles[1:], start=1):
            if always[idx]:
                score(idx, b, t, False)
            else:
                pl.when(key_span(b, t) < query_span)(functools.partial(score, idx, b, t, False))

        m = jnp.max(mx_ref[...], axis=1, keepdims=True)
        mx_ref[...] = jnp.broadcast_to(m, (n, span))

        weigh(0, True)
        for idx, (b, t) in enumerate(tiles[1:], start=1):
            if always[idx]:
                weigh(idx, False)
            else:
                visible = key_span(b, t) < query_span
                pl.when(visible)(functools.partial(weigh, idx, False))
                pl.when(jnp.logical_not(visible))(functools.partial(hide, idx))
        for idx, (b, t) in enumerate(tiles):
            v_ref[idx * span : (idx + 1) * span, :] = kv_refs[b][1, t * span : (t + 1) * span, :]
        width = len(tiles) * span
        acc = jnp.dot(p_ref[:, :width], v_ref[:width, :], preferred_element_type=jnp.float32)
        total = jnp.sum(sm_ref[...], axis=1, keepdims=True)
        result = acc / total
        for h in range(group):
            o_ref[:, h * head_size : (h + 1) * head_size] = result[
                h * span : (h + 1) * span, :
            ].astype(o_ref.dtype)

    early = [(b, 0) for b in range(steps)]
    late = early + [(b, 1) for b in range(steps)]
    pl.when(half == 0)(lambda: run(early, [b == 0 for b, t in early], 0))
    pl.when(half == 1)(lambda: run(late, [t == 0 or b == 0 for b, t in late], steps))


def attend_half(table, where, q2, blocks, *, span, group, head_size, first, count, out_cols, out_block0):
    steps = len(blocks)
    width = group * head_size
    kernel = functools.partial(
        attend_kernel,
        span=span,
        group=group,
        head_size=head_size,
        steps=steps,
        scale=1.0 / head_size**0.5,
    )
    q_spec = pl.BlockSpec((group, span, head_size), lambda g, tb, w: (g + first, w[0], 0))
    kv_spec = pl.BlockSpec((2, 2 * span, head_size), lambda g, tb, w: (0, 0, g + first))
    o_spec = pl.BlockSpec((span, width), lambda g, tb, w: (0, out_block0(w) + g))
    flops = 4 * span * 2 * span * steps * head_size * group * count
    return pl.pallas_call(
        kernel,
        out_shape=jax.ShapeDtypeStruct((span, out_cols), jnp.bfloat16),
        grid_spec=pltpu.PrefetchScalarGridSpec(
            num_scalar_prefetch=2,
            grid=(count,),
            in_specs=[q_spec] + [kv_spec] * steps,
            out_specs=o_spec,
            scratch_shapes=[
                pltpu.VMEM((2 * steps, group * span, span), jnp.float32),
                pltpu.VMEM((group * span, span), jnp.float32),
                pltpu.VMEM((group * span, span), jnp.float32),
                pltpu.VMEM((group * span, 2 * steps * span), jnp.bfloat16),
                pltpu.VMEM((2 * steps * span, head_size), jnp.bfloat16),
            ],
        ),
        compiler_params=pltpu.CompilerParams(dimension_semantics=("arbitrary",)),
        cost_estimate=pl.CostEstimate(
            flops=flops,
            transcendentals=flops // (4 * head_size),
            bytes_accessed=2 * span * width * count * 2 + steps * 2 * 2 * span * count * head_size * 2,
        ),
    )(table, where, q2, *blocks)


def body(queries, key_value, span_table):
    rows = queries.shape[0]
    heads_here = queries.shape[1]
    head_size = queries.shape[2]
    kv_here = key_value.shape[2]
    group = heads_here // kv_here
    span = rows // 2
    cycle = lax.axis_size("ctx")
    myself = lax.axis_index("ctx")
    half = lax.axis_index("kvh")
    table = span_table.reshape(cycle, 2)

    q2 = jnp.transpose(queries, (1, 0, 2))
    own = key_value.reshape(2, rows, kv_here * head_size)
    first = shifted(own, "ctx", 1)
    third = shifted(own, "ctx", 3)
    pairs = [(d, d ^ 1) for d in range(cycle)]
    second = lax.ppermute(jnp.where(myself % 2 == 0, first, third), "ctx", pairs)
    blocks = [own, first, second, third]

    width = heads_here * head_size
    lanes = jnp.arange(2, dtype=jnp.int32)
    sent_where = jnp.where(lanes == 0, 1 - half, myself).astype(jnp.int32)
    kept_where = jnp.where(lanes == 0, half, myself).astype(jnp.int32)
    common = dict(span=span, group=group, head_size=head_size)
    chunks = 1
    per = kv_here // chunks
    arrived = []
    for j in range(chunks):
        sent = attend_half(
            span_table, sent_where, q2, blocks, first=j * per, count=per,
            out_cols=per * group * head_size, out_block0=lambda w: 0, **common,
        )
        arrived.append(shifted(sent, "kvh", 1))
    out = attend_half(
        span_table, kept_where, q2, blocks, first=0, count=kv_here,
        out_cols=2 * width, out_block0=lambda w: w[0] * kv_here, **common,
    )
    for j in range(chunks):
        out = lax.dynamic_update_slice(
            out, arrived[j], (0, (1 - half) * width + j * per * group * head_size)
        )
    return out


def solution(mesh):
    in_specs = (P("ctx", "kvh", None), P(None, "ctx", "kvh", None), P())
    out_specs = P(("ctx", "kvh"), None)
    return jax.shard_map(body, mesh=mesh, in_specs=in_specs, out_specs=out_specs, check_vma=False)
```

```python
import functools

import jax
import jax.numpy as jnp
from jax import lax
from jax.experimental import pallas as pl
from jax.experimental.pallas import tpu as pltpu
from jax.sharding import PartitionSpec as P

STEPS = 4


def shifted(value, axis, steps):
    count = lax.axis_size(axis)
    pairs = [(source, (source + steps) % count) for source in range(count)]
    return lax.ppermute(value, axis, pairs)


def attend_kernel(table_ref, where_ref, q_ref, *refs, span, group, head_size, steps, scale):
    kv_refs = refs[:steps]
    o_ref = refs[steps]
    s_ref, mx_ref, sm_ref, p_ref, v_ref = refs[steps + 1 :]
    cycle = table_ref.shape[0] // 2
    half = where_ref[0]
    myself = where_ref[1]
    query_span = table_ref[2 * myself + half]
    n = group * span

    def key_span(b, t):
        return table_ref[2 * ((myself + cycle - b) % cycle) + t]

    def run(tiles, always, diag):
        def score(idx, b, t, first):
            k = kv_refs[b][0, t * span : (t + 1) * span, :]
            q = q_ref[...].reshape(n, head_size)
            s = jnp.dot(q, k.T, preferred_element_type=jnp.float32) * scale
            if idx == diag:
                row = lax.broadcasted_iota(jnp.int32, (n, span), 0) % span
                col = lax.broadcasted_iota(jnp.int32, (n, span), 1)
                s = jnp.where(col <= row, s, -jnp.inf)
            s_ref[idx] = s
            if first:
                mx_ref[...] = s
            else:
                mx_ref[...] = jnp.maximum(mx_ref[...], s)

        def weigh(idx, first):
            p = jnp.exp(s_ref[idx] - mx_ref[...])
            p_ref[:, idx * span : (idx + 1) * span] = p.astype(jnp.bfloat16)
            if first:
                sm_ref[...] = p
            else:
                sm_ref[...] += p

        def hide(idx):
            p_ref[:, idx * span : (idx + 1) * span] = jnp.zeros((n, span), jnp.bfloat16)

        score(0, *tiles[0], True)
        for idx, (b, t) in enumerate(tiles[1:], start=1):
            if always[idx]:
                score(idx, b, t, False)
            else:
                pl.when(key_span(b, t) < query_span)(functools.partial(score, idx, b, t, False))

        m = jnp.max(mx_ref[...], axis=1, keepdims=True)
        mx_ref[...] = jnp.broadcast_to(m, (n, span))

        weigh(0, True)
        for idx, (b, t) in enumerate(tiles[1:], start=1):
            if always[idx]:
                weigh(idx, False)
            else:
                visible = key_span(b, t) < query_span
                pl.when(visible)(functools.partial(weigh, idx, False))
                pl.when(jnp.logical_not(visible))(functools.partial(hide, idx))
        for idx, (b, t) in enumerate(tiles):
            v_ref[idx * span : (idx + 1) * span, :] = kv_refs[b][1, t * span : (t + 1) * span, :]
        width = len(tiles) * span
        acc = jnp.dot(p_ref[:, :width], v_ref[:width, :], preferred_element_type=jnp.float32)
        total = jnp.sum(sm_ref[...], axis=1, keepdims=True)
        result = acc / total
        for h in range(group):
            o_ref[:, h * head_size : (h + 1) * head_size] = result[
                h * span : (h + 1) * span, :
            ].astype(o_ref.dtype)

    early = [(b, 0) for b in range(steps)]
    late = early + [(b, 1) for b in range(steps)]
    pl.when(half == 0)(lambda: run(early, [b == 0 for b, t in early], 0))
    pl.when(half == 1)(lambda: run(late, [t == 0 or b == 0 for b, t in late], steps))


def attend_half(table, where, q2, blocks, *, span, group, head_size, first, count, out_cols, out_block0):
    steps = len(blocks)
    width = group * head_size
    kernel = functools.partial(
        attend_kernel,
        span=span,
        group=group,
        head_size=head_size,
        steps=steps,
        scale=1.0 / head_size**0.5,
    )
    q_spec = pl.BlockSpec((group, span, head_size), lambda g, tb, w: (g + first, w[0], 0))
    kv_spec = pl.BlockSpec((2, 2 * span, head_size), lambda g, tb, w: (0, 0, g + first))
    o_spec = pl.BlockSpec((span, width), lambda g, tb, w: (0, out_block0(w) + g))
    flops = 4 * span * 2 * span * steps * head_size * group * count
    return pl.pallas_call(
        kernel,
        out_shape=jax.ShapeDtypeStruct((span, out_cols), jnp.bfloat16),
        grid_spec=pltpu.PrefetchScalarGridSpec(
            num_scalar_prefetch=2,
            grid=(count,),
            in_specs=[q_spec] + [kv_spec] * steps,
            out_specs=o_spec,
            scratch_shapes=[
                pltpu.VMEM((2 * steps, group * span, span), jnp.float32),
                pltpu.VMEM((group * span, span), jnp.float32),
                pltpu.VMEM((group * span, span), jnp.float32),
                pltpu.VMEM((group * span, 2 * steps * span), jnp.bfloat16),
                pltpu.VMEM((2 * steps * span, head_size), jnp.bfloat16),
            ],
        ),
        compiler_params=pltpu.CompilerParams(dimension_semantics=("arbitrary",)),
        cost_estimate=pl.CostEstimate(
            flops=flops,
            transcendentals=flops // (4 * head_size),
            bytes_accessed=2 * span * width * count * 2 + steps * 2 * 2 * span * count * head_size * 2,
        ),
    )(table, where, q2, *blocks)


def body(queries, key_value, span_table):
    rows = queries.shape[0]
    heads_here = queries.shape[1]
    head_size = queries.shape[2]
    kv_here = key_value.shape[2]
    group = heads_here // kv_here
    span = rows // 2
    cycle = lax.axis_size("ctx")
    myself = lax.axis_index("ctx")
    half = lax.axis_index("kvh")
    table = span_table.reshape(cycle, 2)

    own = key_value.reshape(2, rows, kv_here * head_size)
    first = shifted(own, "ctx", 1)
    third = shifted(own, "ctx", 3)
    queries, third = lax.optimization_barrier((queries, third))
    q2 = jnp.transpose(queries, (1, 0, 2))
    first, q2 = lax.optimization_barrier((first, q2))
    pairs = [(d, d ^ 1) for d in range(cycle)]
    second = lax.ppermute(jnp.where(myself % 2 == 0, first, third), "ctx", pairs)
    blocks = [own, first, second, third]

    width = heads_here * head_size
    lanes = jnp.arange(2, dtype=jnp.int32)
    sent_where = jnp.where(lanes == 0, 1 - half, myself).astype(jnp.int32)
    kept_where = jnp.where(lanes == 0, half, myself).astype(jnp.int32)
    common = dict(span=span, group=group, head_size=head_size)
    chunks = 2
    per = kv_here // chunks
    arrived = []
    for j in range(chunks):
        sent = attend_half(
            span_table, sent_where, q2, blocks, first=j * per, count=per,
            out_cols=per * group * head_size, out_block0=lambda w: 0, **common,
        )
        arrived.append(shifted(sent, "kvh", 1))
    out = attend_half(
        span_table, kept_where, q2, blocks, first=0, count=kv_here,
        out_cols=2 * width, out_block0=lambda w: w[0] * kv_here, **common,
    )
    for j in range(chunks):
        out = lax.dynamic_update_slice(
            out, arrived[j], (0, (1 - half) * width + j * per * group * head_size)
        )
    return out


def solution(mesh):
    in_specs = (P("ctx", "kvh", None), P(None, "ctx", "kvh", None), P())
    out_specs = P(("ctx", "kvh"), None)
    return jax.shard_map(body, mesh=mesh, in_specs=in_specs, out_specs=out_specs, check_vma=False)
```

```python
import functools

import jax
import jax.numpy as jnp
from jax import lax
from jax.experimental import pallas as pl
from jax.experimental.pallas import tpu as pltpu
from jax.sharding import PartitionSpec as P

STEPS = 4


def shifted(value, axis, steps):
    count = lax.axis_size(axis)
    pairs = [(source, (source + steps) % count) for source in range(count)]
    return lax.ppermute(value, axis, pairs)


def attend_kernel(table_ref, where_ref, q_ref, *refs, span, group, head_size, steps, scale):
    kv_refs = refs[:steps]
    o_ref = refs[steps]
    s_ref, mx_ref, sm_ref, p_ref, v_ref = refs[steps + 1 :]
    cycle = table_ref.shape[0] // 2
    half = where_ref[0]
    myself = where_ref[1]
    query_span = table_ref[2 * myself + half]
    n = group * span

    def key_span(b, t):
        return table_ref[2 * ((myself + cycle - b) % cycle) + t]

    def run(tiles, always, diag):
        def score(idx, b, t, first):
            k = kv_refs[b][0, t * span : (t + 1) * span, :]
            q = q_ref[...].reshape(n, head_size)
            s = jnp.dot(q, k.T, preferred_element_type=jnp.float32) * scale
            if idx == diag:
                row = lax.broadcasted_iota(jnp.int32, (n, span), 0) % span
                col = lax.broadcasted_iota(jnp.int32, (n, span), 1)
                s = jnp.where(col <= row, s, -jnp.inf)
            s_ref[idx] = s
            if first:
                mx_ref[...] = s
            else:
                mx_ref[...] = jnp.maximum(mx_ref[...], s)

        def weigh(idx, first):
            p = jnp.exp(s_ref[idx] - mx_ref[...])
            p_ref[:, idx * span : (idx + 1) * span] = p.astype(jnp.bfloat16)
            if first:
                sm_ref[...] = p
            else:
                sm_ref[...] += p

        def hide(idx):
            p_ref[:, idx * span : (idx + 1) * span] = jnp.zeros((n, span), jnp.bfloat16)

        score(0, *tiles[0], True)
        for idx, (b, t) in enumerate(tiles[1:], start=1):
            if always[idx]:
                score(idx, b, t, False)
            else:
                pl.when(key_span(b, t) < query_span)(functools.partial(score, idx, b, t, False))

        m = jnp.max(mx_ref[...], axis=1, keepdims=True)
        mx_ref[...] = jnp.broadcast_to(m, (n, span))

        weigh(0, True)
        for idx, (b, t) in enumerate(tiles[1:], start=1):
            if always[idx]:
                weigh(idx, False)
            else:
                visible = key_span(b, t) < query_span
                pl.when(visible)(functools.partial(weigh, idx, False))
                pl.when(jnp.logical_not(visible))(functools.partial(hide, idx))
        for idx, (b, t) in enumerate(tiles):
            v_ref[idx * span : (idx + 1) * span, :] = kv_refs[b][1, t * span : (t + 1) * span, :]
        width = len(tiles) * span
        acc = jnp.dot(p_ref[:, :width], v_ref[:width, :], preferred_element_type=jnp.float32)
        total = jnp.sum(sm_ref[...], axis=1, keepdims=True)
        result = acc / total
        for h in range(group):
            o_ref[:, h * head_size : (h + 1) * head_size] = result[
                h * span : (h + 1) * span, :
            ].astype(o_ref.dtype)

    early = [(b, 0) for b in range(steps)]
    late = early + [(b, 1) for b in range(steps)]
    pl.when(half == 0)(lambda: run(early, [b == 0 for b, t in early], 0))
    pl.when(half == 1)(lambda: run(late, [t == 0 or b == 0 for b, t in late], steps))


def attend_half(table, where, q2, blocks, *, span, group, head_size, first, count, out_cols, out_block0):
    steps = len(blocks)
    width = group * head_size
    kernel = functools.partial(
        attend_kernel,
        span=span,
        group=group,
        head_size=head_size,
        steps=steps,
        scale=1.0 / head_size**0.5,
    )
    q_spec = pl.BlockSpec((group, span, head_size), lambda g, tb, w: (g + first, w[0], 0))
    kv_spec = pl.BlockSpec((2, 2 * span, head_size), lambda g, tb, w: (0, 0, g + first))
    o_spec = pl.BlockSpec((span, width), lambda g, tb, w: (0, out_block0(w) + g))
    flops = 4 * span * 2 * span * steps * head_size * group * count
    return pl.pallas_call(
        kernel,
        out_shape=jax.ShapeDtypeStruct((span, out_cols), jnp.bfloat16),
        grid_spec=pltpu.PrefetchScalarGridSpec(
            num_scalar_prefetch=2,
            grid=(count,),
            in_specs=[q_spec] + [kv_spec] * steps,
            out_specs=o_spec,
            scratch_shapes=[
                pltpu.VMEM((2 * steps, group * span, span), jnp.float32),
                pltpu.VMEM((group * span, span), jnp.float32),
                pltpu.VMEM((group * span, span), jnp.float32),
                pltpu.VMEM((group * span, 2 * steps * span), jnp.bfloat16),
                pltpu.VMEM((2 * steps * span, head_size), jnp.bfloat16),
            ],
        ),
        compiler_params=pltpu.CompilerParams(dimension_semantics=("arbitrary",)),
        cost_estimate=pl.CostEstimate(
            flops=flops,
            transcendentals=flops // (4 * head_size),
            bytes_accessed=2 * span * width * count * 2 + steps * 2 * 2 * span * count * head_size * 2,
        ),
    )(table, where, q2, *blocks)


def body(queries, key_value, span_table):
    rows = queries.shape[0]
    heads_here = queries.shape[1]
    head_size = queries.shape[2]
    kv_here = key_value.shape[2]
    group = heads_here // kv_here
    span = rows // 2
    cycle = lax.axis_size("ctx")
    myself = lax.axis_index("ctx")
    half = lax.axis_index("kvh")
    table = span_table.reshape(cycle, 2)

    own = key_value.reshape(2, rows, kv_here * head_size)
    first = shifted(own, "ctx", 1)
    third = shifted(own, "ctx", 3)
    queries, third = lax.optimization_barrier((queries, third))
    q2 = jnp.transpose(queries, (1, 0, 2))
    lanes = jnp.arange(2, dtype=jnp.int32)
    sent_where = jnp.where(lanes == 0, 1 - half, myself).astype(jnp.int32)
    kept_where = jnp.where(lanes == 0, half, myself).astype(jnp.int32)
    first, q2, sent_where, kept_where = lax.optimization_barrier((first, q2, sent_where, kept_where))
    pairs = [(d, d ^ 1) for d in range(cycle)]
    second = lax.ppermute(jnp.where(myself % 2 == 0, first, third), "ctx", pairs)
    blocks = [own, first, second, third]

    width = heads_here * head_size
    common = dict(span=span, group=group, head_size=head_size)
    chunks = 2
    per = kv_here // chunks
    arrived = []
    for j in range(chunks):
        sent = attend_half(
            span_table, sent_where, q2, blocks, first=j * per, count=per,
            out_cols=per * group * head_size, out_block0=lambda w: 0, **common,
        )
        arrived.append(shifted(sent, "kvh", 1))
    out = attend_half(
        span_table, kept_where, q2, blocks, first=0, count=kv_here,
        out_cols=2 * width, out_block0=lambda w: w[0] * kv_here, **common,
    )
    for j in range(chunks):
        out = lax.dynamic_update_slice(
            out, arrived[j], (0, (1 - half) * width + j * per * group * head_size)
        )
    return out


def solution(mesh):
    in_specs = (P("ctx", "kvh", None), P(None, "ctx", "kvh", None), P())
    out_specs = P(("ctx", "kvh"), None)
    return jax.shard_map(body, mesh=mesh, in_specs=in_specs, out_specs=out_specs, check_vma=False)
```

```python
import functools

import jax
import jax.numpy as jnp
from jax import lax
from jax.experimental import pallas as pl
from jax.experimental.pallas import tpu as pltpu
from jax.sharding import PartitionSpec as P

STEPS = 4


def shifted(value, axis, steps):
    count = lax.axis_size(axis)
    pairs = [(source, (source + steps) % count) for source in range(count)]
    return lax.ppermute(value, axis, pairs)


def attend_kernel(table_ref, where_ref, q_ref, *refs, span, group, head_size, steps, scale):
    kv_refs = refs[:steps]
    o_ref = refs[steps]
    s_ref, mx_ref, sm_ref, p_ref, v_ref, qf_ref = refs[steps + 1 :]
    cycle = table_ref.shape[0] // 2
    half = where_ref[0]
    myself = where_ref[1]
    query_span = table_ref[2 * myself + half]
    n = group * span

    def key_span(b, t):
        return table_ref[2 * ((myself + cycle - b) % cycle) + t]

    for h in range(group):
        qf_ref[h * span : (h + 1) * span, :] = q_ref[:, h, :]

    def run(tiles, always, diag):
        def score(idx, b, t, first):
            k = kv_refs[b][0, t * span : (t + 1) * span, :]
            q = qf_ref[...]
            s = jnp.dot(q, k.T, preferred_element_type=jnp.float32) * scale
            if idx == diag:
                row = lax.broadcasted_iota(jnp.int32, (n, span), 0) % span
                col = lax.broadcasted_iota(jnp.int32, (n, span), 1)
                s = jnp.where(col <= row, s, -jnp.inf)
            s_ref[idx] = s
            if first:
                mx_ref[...] = s
            else:
                mx_ref[...] = jnp.maximum(mx_ref[...], s)

        def weigh(idx, first):
            p = jnp.exp(s_ref[idx] - mx_ref[...])
            p_ref[:, idx * span : (idx + 1) * span] = p.astype(jnp.bfloat16)
            if first:
                sm_ref[...] = p
            else:
                sm_ref[...] += p

        def hide(idx):
            p_ref[:, idx * span : (idx + 1) * span] = jnp.zeros((n, span), jnp.bfloat16)

        score(0, *tiles[0], True)
        for idx, (b, t) in enumerate(tiles[1:], start=1):
            if always[idx]:
                score(idx, b, t, False)
            else:
                pl.when(key_span(b, t) < query_span)(functools.partial(score, idx, b, t, False))

        m = jnp.max(mx_ref[...], axis=1, keepdims=True)
        mx_ref[...] = jnp.broadcast_to(m, (n, span))

        weigh(0, True)
        for idx, (b, t) in enumerate(tiles[1:], start=1):
            if always[idx]:
                weigh(idx, False)
            else:
                visible = key_span(b, t) < query_span
                pl.when(visible)(functools.partial(weigh, idx, False))
                pl.when(jnp.logical_not(visible))(functools.partial(hide, idx))
        for idx, (b, t) in enumerate(tiles):
            v_ref[idx * span : (idx + 1) * span, :] = kv_refs[b][1, t * span : (t + 1) * span, :]
        width = len(tiles) * span
        acc = jnp.dot(p_ref[:, :width], v_ref[:width, :], preferred_element_type=jnp.float32)
        total = jnp.sum(sm_ref[...], axis=1, keepdims=True)
        result = acc / total
        for h in range(group):
            o_ref[:, h * head_size : (h + 1) * head_size] = result[
                h * span : (h + 1) * span, :
            ].astype(o_ref.dtype)

    early = [(b, 0) for b in range(steps)]
    late = early + [(b, 1) for b in range(steps)]
    pl.when(half == 0)(lambda: run(early, [b == 0 for b, t in early], 0))
    pl.when(half == 1)(lambda: run(late, [t == 0 or b == 0 for b, t in late], steps))


def attend_half(table, where, q2, blocks, *, span, group, head_size, first, count, out_cols, out_block0):
    steps = len(blocks)
    width = group * head_size
    kernel = functools.partial(
        attend_kernel,
        span=span,
        group=group,
        head_size=head_size,
        steps=steps,
        scale=1.0 / head_size**0.5,
    )
    q_spec = pl.BlockSpec((span, group, head_size), lambda g, tb, w: (w[0], g + first, 0))
    kv_spec = pl.BlockSpec((2, 2 * span, head_size), lambda g, tb, w: (0, 0, g + first))
    o_spec = pl.BlockSpec((span, width), lambda g, tb, w: (0, out_block0(w) + g))
    flops = 4 * span * 2 * span * steps * head_size * group * count
    return pl.pallas_call(
        kernel,
        out_shape=jax.ShapeDtypeStruct((span, out_cols), jnp.bfloat16),
        grid_spec=pltpu.PrefetchScalarGridSpec(
            num_scalar_prefetch=2,
            grid=(count,),
            in_specs=[q_spec] + [kv_spec] * steps,
            out_specs=o_spec,
            scratch_shapes=[
                pltpu.VMEM((2 * steps, group * span, span), jnp.float32),
                pltpu.VMEM((group * span, span), jnp.float32),
                pltpu.VMEM((group * span, span), jnp.float32),
                pltpu.VMEM((group * span, 2 * steps * span), jnp.bfloat16),
                pltpu.VMEM((2 * steps * span, head_size), jnp.bfloat16),
                pltpu.VMEM((group * span, head_size), jnp.bfloat16),
            ],
        ),
        compiler_params=pltpu.CompilerParams(dimension_semantics=("arbitrary",)),
        cost_estimate=pl.CostEstimate(
            flops=flops,
            transcendentals=flops // (4 * head_size),
            bytes_accessed=2 * span * width * count * 2 + steps * 2 * 2 * span * count * head_size * 2,
        ),
    )(table, where, q2, *blocks)


def body(queries, key_value, span_table):
    rows = queries.shape[0]
    heads_here = queries.shape[1]
    head_size = queries.shape[2]
    kv_here = key_value.shape[2]
    group = heads_here // kv_here
    span = rows // 2
    cycle = lax.axis_size("ctx")
    myself = lax.axis_index("ctx")
    half = lax.axis_index("kvh")
    table = span_table.reshape(cycle, 2)

    own = key_value.reshape(2, rows, kv_here * head_size)
    first = shifted(own, "ctx", 1)
    third = shifted(own, "ctx", 3)
    q2 = queries
    lanes = jnp.arange(2, dtype=jnp.int32)
    sent_where = jnp.where(lanes == 0, 1 - half, myself).astype(jnp.int32)
    kept_where = jnp.where(lanes == 0, half, myself).astype(jnp.int32)
    first, q2, sent_where, kept_where = lax.optimization_barrier((first, q2, sent_where, kept_where))
    pairs = [(d, d ^ 1) for d in range(cycle)]
    second = lax.ppermute(jnp.where(myself % 2 == 0, first, third), "ctx", pairs)
    blocks = [own, first, second, third]

    width = heads_here * head_size
    common = dict(span=span, group=group, head_size=head_size)
    chunks = 2
    per = kv_here // chunks
    arrived = []
    for j in range(chunks):
        sent = attend_half(
            span_table, sent_where, q2, blocks, first=j * per, count=per,
            out_cols=per * group * head_size, out_block0=lambda w: 0, **common,
        )
        arrived.append(shifted(sent, "kvh", 1))
    out = attend_half(
        span_table, kept_where, q2, blocks, first=0, count=kv_here,
        out_cols=2 * width, out_block0=lambda w: w[0] * kv_here, **common,
    )
    for j in range(chunks):
        out = lax.dynamic_update_slice(
            out, arrived[j], (0, (1 - half) * width + j * per * group * head_size)
        )
    return out


def solution(mesh):
    in_specs = (P("ctx", "kvh", None), P(None, "ctx", "kvh", None), P())
    out_specs = P(("ctx", "kvh"), None)
    return jax.shard_map(body, mesh=mesh, in_specs=in_specs, out_specs=out_specs, check_vma=False)
```

```python
import functools

import jax
import jax.numpy as jnp
from jax import lax
from jax.experimental import pallas as pl
from jax.experimental.pallas import tpu as pltpu
from jax.sharding import PartitionSpec as P

STEPS = 4


def shifted(value, axis, steps):
    count = lax.axis_size(axis)
    pairs = [(source, (source + steps) % count) for source in range(count)]
    return lax.ppermute(value, axis, pairs)


def attend_kernel(table_ref, where_ref, q_ref, *refs, span, group, head_size, steps, scale):
    kv_refs = refs[:steps]
    o_ref = refs[steps]
    s_ref, mx_ref, sm_ref, p_ref, v_ref = refs[steps + 1 :]
    cycle = table_ref.shape[0] // 2
    half = where_ref[0]
    myself = where_ref[1]
    query_span = table_ref[2 * myself + half]
    n = group * span

    def key_span(b, t):
        return table_ref[2 * ((myself + cycle - b) % cycle) + t]

    def run(tiles, always, diag):
        def score(idx, b, t, first):
            k = kv_refs[b][0, t * span : (t + 1) * span, :]
            q = q_ref[...].reshape(n, head_size)
            s = jnp.dot(q, k.T, preferred_element_type=jnp.float32) * scale
            if idx == diag:
                row = lax.broadcasted_iota(jnp.int32, (n, span), 0) % span
                col = lax.broadcasted_iota(jnp.int32, (n, span), 1)
                s = jnp.where(col <= row, s, -jnp.inf)
            s_ref[idx] = s
            if first:
                mx_ref[...] = s
            else:
                mx_ref[...] = jnp.maximum(mx_ref[...], s)

        def weigh(idx, first, m):
            p = jnp.exp(s_ref[idx] - m)
            p_ref[:, idx * span : (idx + 1) * span] = p.astype(jnp.bfloat16)
            if first:
                sm_ref[...] = p
            else:
                sm_ref[...] += p

        def hide(idx):
            p_ref[:, idx * span : (idx + 1) * span] = jnp.zeros((n, span), jnp.bfloat16)

        score(0, *tiles[0], True)
        for idx, (b, t) in enumerate(tiles[1:], start=1):
            if always[idx]:
                score(idx, b, t, False)
            else:
                pl.when(key_span(b, t) < query_span)(functools.partial(score, idx, b, t, False))

        m = jnp.max(mx_ref[...], axis=1, keepdims=True)

        weigh(0, True, m)
        for idx, (b, t) in enumerate(tiles[1:], start=1):
            if always[idx]:
                weigh(idx, False, m)
            else:
                visible = key_span(b, t) < query_span
                pl.when(visible)(functools.partial(weigh, idx, False, m))
                pl.when(jnp.logical_not(visible))(functools.partial(hide, idx))
        for idx, (b, t) in enumerate(tiles):
            v_ref[idx * span : (idx + 1) * span, :] = kv_refs[b][1, t * span : (t + 1) * span, :]
        width = len(tiles) * span
        acc = jnp.dot(p_ref[:, :width], v_ref[:width, :], preferred_element_type=jnp.float32)
        total = jnp.sum(sm_ref[...], axis=1, keepdims=True)
        result = acc / total
        for h in range(group):
            o_ref[:, h * head_size : (h + 1) * head_size] = result[
                h * span : (h + 1) * span, :
            ].astype(o_ref.dtype)

    early = [(b, 0) for b in range(steps)]
    late = early + [(b, 1) for b in range(steps)]
    pl.when(half == 0)(lambda: run(early, [b == 0 for b, t in early], 0))
    pl.when(half == 1)(lambda: run(late, [t == 0 or b == 0 for b, t in late], steps))


def attend_half(table, where, q2, blocks, *, span, group, head_size, first, count, out_cols, out_block0):
    steps = len(blocks)
    width = group * head_size
    kernel = functools.partial(
        attend_kernel,
        span=span,
        group=group,
        head_size=head_size,
        steps=steps,
        scale=1.0 / head_size**0.5,
    )
    q_spec = pl.BlockSpec((group, span, head_size), lambda g, tb, w: (g + first, w[0], 0))
    kv_spec = pl.BlockSpec((2, 2 * span, head_size), lambda g, tb, w: (0, 0, g + first))
    o_spec = pl.BlockSpec((span, width), lambda g, tb, w: (0, out_block0(w) + g))
    flops = 4 * span * 2 * span * steps * head_size * group * count
    return pl.pallas_call(
        kernel,
        out_shape=jax.ShapeDtypeStruct((span, out_cols), jnp.bfloat16),
        grid_spec=pltpu.PrefetchScalarGridSpec(
            num_scalar_prefetch=2,
            grid=(count,),
            in_specs=[q_spec] + [kv_spec] * steps,
            out_specs=o_spec,
            scratch_shapes=[
                pltpu.VMEM((2 * steps, group * span, span), jnp.float32),
                pltpu.VMEM((group * span, span), jnp.float32),
                pltpu.VMEM((group * span, span), jnp.float32),
                pltpu.VMEM((group * span, 2 * steps * span), jnp.bfloat16),
                pltpu.VMEM((2 * steps * span, head_size), jnp.bfloat16),
            ],
        ),
        compiler_params=pltpu.CompilerParams(dimension_semantics=("arbitrary",)),
        cost_estimate=pl.CostEstimate(
            flops=flops,
            transcendentals=flops // (4 * head_size),
            bytes_accessed=2 * span * width * count * 2 + steps * 2 * 2 * span * count * head_size * 2,
        ),
    )(table, where, q2, *blocks)


def body(queries, key_value, span_table):
    rows = queries.shape[0]
    heads_here = queries.shape[1]
    head_size = queries.shape[2]
    kv_here = key_value.shape[2]
    group = heads_here // kv_here
    span = rows // 2
    cycle = lax.axis_size("ctx")
    myself = lax.axis_index("ctx")
    half = lax.axis_index("kvh")
    table = span_table.reshape(cycle, 2)

    own = key_value.reshape(2, rows, kv_here * head_size)
    first = shifted(own, "ctx", 1)
    third = shifted(own, "ctx", 3)
    queries, third = lax.optimization_barrier((queries, third))
    q2 = jnp.transpose(queries, (1, 0, 2))
    lanes = jnp.arange(2, dtype=jnp.int32)
    sent_where = jnp.where(lanes == 0, 1 - half, myself).astype(jnp.int32)
    kept_where = jnp.where(lanes == 0, half, myself).astype(jnp.int32)
    first, q2, sent_where, kept_where = lax.optimization_barrier((first, q2, sent_where, kept_where))
    pairs = [(d, d ^ 1) for d in range(cycle)]
    second = lax.ppermute(jnp.where(myself % 2 == 0, first, third), "ctx", pairs)
    blocks = [own, first, second, third]

    width = heads_here * head_size
    common = dict(span=span, group=group, head_size=head_size)
    chunks = 2
    per = kv_here // chunks
    arrived = []
    for j in range(chunks):
        sent = attend_half(
            span_table, sent_where, q2, blocks, first=j * per, count=per,
            out_cols=per * group * head_size, out_block0=lambda w: 0, **common,
        )
        arrived.append(shifted(sent, "kvh", 1))
    out = attend_half(
        span_table, kept_where, q2, blocks, first=0, count=kv_here,
        out_cols=2 * width, out_block0=lambda w: w[0] * kv_here, **common,
    )
    for j in range(chunks):
        out = lax.dynamic_update_slice(
            out, arrived[j], (0, (1 - half) * width + j * per * group * head_size)
        )
    return out


def solution(mesh):
    in_specs = (P("ctx", "kvh", None), P(None, "ctx", "kvh", None), P())
    out_specs = P(("ctx", "kvh"), None)
    return jax.shard_map(body, mesh=mesh, in_specs=in_specs, out_specs=out_specs, check_vma=False)
```
